128 devices in a mesh: grid: 32 (over x, y, core), orb: 4 (over z).
Axes of the slice: x: 4, y: 4, z: 4, core: 2. Of those that a mesh axis runs over, the one named last changes fastest.
Arguments:
- orbital_block: float32 [128, 192, 48, 128], P('orb', 'grid'), may hold values from -30 to 30
- potential: float32 [192, 48, 128], P('grid'), may hold values from -6 to -0.5
Outputs:
- orbitals: float32 [128, 192, 48, 128], P('orb', 'grid')
- triangle: float32 [128, 128], replicated
The draws below stay inside these ranges and needn't reach their ends.
All inputs are finite; a program needn't handle non-finite values.
Results may differ from the reference program's by a relative error of at most 0.0003.
Values sent between devices are 32-bit elements; how exact they have to be, the bound alone decides.
No kernel may reach another device: no remote copies, remote signals or barrier semaphores. Data moves between devices by JAX's collectives and lax.ppermute only.
A program may use at most 128 MiB of HBM per device.

```python
import math
import jax
import jax.numpy as jnp
from jax import lax

NORB = 128
NY = 48
NZ = 128
NX = 192


def draw_orbital_block(key, part):
    subkeys = jax.random.split(key, 2)
    extent = (NORB, NX, NY, NZ)
    position = lax.broadcasted_iota(jnp.float32, (1, NX, 1, 1), 1) / max(NX - 1, 1)
    amplitude = jnp.exp(jax.random.uniform(subkeys[0], (1, NX, NY, NZ)) * math.log(3.2))
    growth = 1.0 + 0.75 * position
    samples = jax.random.truncated_normal(subkeys[1], -4.0, 4.0, extent)
    return (samples * amplitude * growth).astype(jnp.float32)


def steps_of(key, shape, pieces, low, top_value):
    factor_of = 1.0
    for dim, blocks in pieces:
        heights = jax.random.uniform(jax.random.fold_in(jax.random.fold_in(key, 6), dim), (blocks,), jnp.float32, low / len(pieces), top_value / len(pieces))
        factor_of = factor_of * jnp.repeat(jnp.exp(heights), shape[dim] // blocks).reshape((-1,) + (1,) * (len(shape) - 1 - dim))
    return factor_of


def setup_inputs(seed: int = 0) -> dict:
    streams_of = jax.random.split(jax.random.key(seed), 3)
    orbital_block = draw_orbital_block(jax.random.fold_in(streams_of[2], 71), 0)
    potential = jnp.clip(-6.0 + 5.5 * jax.random.uniform(streams_of[1], (NX, NY, NZ), jnp.float32) ** steps_of(streams_of[1], (NX, NY, NZ), ((0, 32),), -0.2, 0.2), -6.0, -0.5)
    return dict(orbital_block=orbital_block, potential=potential)


coefs = (-5369.0 / 1800.0, 12.0 / 7.0, -15.0 / 56.0, 10.0 / 189.0, -1.0 / 112.0, 2.0 / 1925.0, -1.0 / 16632.0)
centre = 23.5
radius = 19.5

def hamiltonian(orbital_field, potential):
    extent_x, extent_y, extent_z = orbital_field.shape
    padded = jnp.pad(orbital_field, 6)
    total = 3.0 * coefs[0] * orbital_field
    for k in range(1, 7):
        total = total + coefs[k] * (padded[6 + k:6 + k + extent_x, 6:6 + extent_y, 6:6 + extent_z] + padded[6 - k:6 - k + extent_x, 6:6 + extent_y, 6:6 + extent_z])
        total = total + coefs[k] * (padded[6:6 + extent_x, 6 + k:6 + k + extent_y, 6:6 + extent_z] + padded[6:6 + extent_x, 6 - k:6 - k + extent_y, 6:6 + extent_z])
        total = total + coefs[k] * (padded[6:6 + extent_x, 6:6 + extent_y, 6 + k:6 + k + extent_z] + padded[6:6 + extent_x, 6:6 + extent_y, 6 - k:6 - k + extent_z])
    return -2.0 * total + potential * orbital_field

def filter_one(orbital_field, potential):
    first = (hamiltonian(orbital_field, potential) - centre * orbital_field) / radius
    return 2.0 * (hamiltonian(first, potential) - centre * first) / radius - orbital_field

def reference(orbital_block, potential):
    filtered = lax.map(lambda single: filter_one(single, potential), orbital_block)
    filtered = filtered.reshape(NORB, NX * NY * NZ)
    q, r = jnp.linalg.qr(filtered.T)
    sign_fix = jnp.sign(jnp.diagonal(r))
    root_cells = math.sqrt(NX * NY * NZ)
    triangle = r * sign_fix[:, None] / root_cells
    orbitals = (q * sign_fix[None, :]).T * root_cells
    return (orbitals.reshape(orbital_block.shape), triangle)
```

```python
import jax
import jax.numpy as jnp
from jax import lax
from jax.experimental import pallas as pl
from jax.experimental.pallas import tpu as pltpu
from jax.sharding import PartitionSpec as P

coefs = (
    -5369.0 / 1800.0,
    12.0 / 7.0,
    -15.0 / 56.0,
    10.0 / 189.0,
    -1.0 / 112.0,
    2.0 / 1925.0,
    -1.0 / 16632.0,
)
centre = 23.5
radius = 19.5
highest = lax.Precision.HIGHEST


def padded_2(value, sides, width):
    for axis, dim in sides:
        size, length = (lax.axis_size(axis), value.shape[dim])
        up = [(i, (i + 1) % size) for i in range(size - 1)]
        down = [(j, i) for i, j in up]
        last = lax.slice_in_dim(value, length - width, length, axis=dim)
        first = lax.slice_in_dim(value, 0, width, axis=dim)
        before = lax.ppermute(last, axis, up)
        after = lax.ppermute(first, axis, down)
        value = jnp.concatenate([before, value, after], axis=dim)
    return value


def hamiltonian(orbital_field, potential):
    slab_cells = orbital_field.shape[1]
    across = orbital_field.shape[2]
    depth_cells = orbital_field.shape[3]
    widened = padded_2(orbital_field, (("grid", 1),), 6)
    padded = jnp.pad(orbital_field, ((0, 0), (0, 0), (6, 6), (6, 6)))
    total = 3.0 * coefs[0] * orbital_field
    for k in range(1, 7):
        total = total + coefs[k] * (
            widened[:, 6 + k : 6 + k + slab_cells] + widened[:, 6 - k : 6 - k + slab_cells]
        )
        total = total + coefs[k] * (
            padded[:, :, 6 + k : 6 + k + across, 6 : 6 + depth_cells]
            + padded[:, :, 6 - k : 6 - k + across, 6 : 6 + depth_cells]
        )
        total = total + coefs[k] * (
            padded[:, :, 6 : 6 + across, 6 + k : 6 + k + depth_cells]
            + padded[:, :, 6 : 6 + across, 6 - k : 6 - k + depth_cells]
        )
    return -2.0 * total + potential[None] * orbital_field


def gram_matrix(left_rows, right_rows):
    return lax.dot_general(
        left_rows,
        right_rows,
        (((1,), (1,)), ((), ())),
        precision=highest,
        preferred_element_type=jnp.float32,
    )


def apply_rows(inverse, source_rows):
    return lax.dot_general(
        inverse,
        source_rows,
        (((0,), (0,)), ((), ())),
        precision=highest,
        preferred_element_type=jnp.float32,
    )


def mix_rows(weights, source_rows):
    return lax.dot_general(
        weights,
        source_rows,
        (((1,), (0,)), ((), ())),
        precision=highest,
        preferred_element_type=jnp.float32,
    )


def exchange_sum(value, axis):
    size = lax.axis_size(axis)
    if size & (size - 1):
        return lax.psum(value, axis)
    step = 1
    while step < size:
        pairs = [(i, i ^ step) for i in range(size)]
        value = value + lax.ppermute(value, axis, pairs)
        step *= 2
    return value


def eliminate_kernel(source_ref, result_ref):
    result_ref[...] = source_ref[...]
    rows, width = result_ref.shape
    lanes = lax.broadcasted_iota(jnp.int32, (1, width), 1)
    cols = lax.broadcasted_iota(jnp.int32, (rows, width), 1)
    row_ids = lax.broadcasted_iota(jnp.int32, (rows, 1), 0)

    def column_step(column, carry):
        current = result_ref[pl.ds(column, 1), :]
        pivot_value = jnp.sum(jnp.where(lanes == column, current, 0.0), axis=1, keepdims=True)
        root = jnp.sqrt(pivot_value)
        scaled = jnp.where(lanes >= column, current, 0.0) / root
        whole = result_ref[...]
        below = jnp.sum(jnp.where(cols == column, whole, 0.0), axis=1, keepdims=True) / root
        below = jnp.where(row_ids > column, below, 0.0)
        whole = whole - below * scaled
        result_ref[...] = jnp.where(row_ids == column, scaled, whole)
        return carry

    lax.fori_loop(0, rows, column_step, 0)


def eliminate(matrix, extra):
    source = jnp.concatenate([matrix, extra], axis=1)
    return pl.pallas_call(
        eliminate_kernel,
        out_shape=jax.ShapeDtypeStruct(source.shape, jnp.float32),
    )(source)


def factorize(rows_block, inv_cells):
    panel_rows = rows_block.shape[0] // 2
    leading = exchange_sum(gram_matrix(rows_block[:panel_rows], rows_block), "grid") * inv_cells
    eye = jnp.eye(panel_rows, dtype=jnp.float32)
    first = eliminate(leading, eye)
    first_r = first[:, :panel_rows]
    coupling = first[:, panel_rows : 2 * panel_rows]
    first_lower_inv = first[:, 2 * panel_rows :]
    first_q = mix_rows(first_lower_inv, rows_block[:panel_rows])
    remainder = rows_block[panel_rows:] - apply_rows(coupling, first_q)
    trailing = exchange_sum(gram_matrix(remainder, remainder), "grid") * inv_cells
    second = eliminate(trailing, eye)
    second_r = second[:, :panel_rows]
    second_lower_inv = second[:, panel_rows:]
    upper_rows = jnp.concatenate([first_r, coupling], axis=1)
    lower_rows = jnp.concatenate(
        [jnp.zeros((second_r.shape[0], panel_rows), jnp.float32), second_r], axis=1
    )
    triangle = jnp.concatenate([upper_rows, lower_rows], axis=0)
    return triangle, first_q, second_lower_inv, remainder


def local(orbital_block, potential):
    orb_rows = orbital_block.shape[0]
    first = (hamiltonian(orbital_block, potential) - centre * orbital_block) / radius
    filtered = 2.0 * (hamiltonian(first, potential) - centre * first) / radius - orbital_block
    filtered = filtered.reshape(orb_rows, -1)
    inv_cells = 1.0 / (lax.axis_size("grid") * filtered.shape[1])
    gathered = lax.all_gather(filtered, "orb", axis=0, tiled=True)
    triangle, first_q, second_lower_inv, remainder = factorize(gathered, inv_cells)
    second_q = mix_rows(second_lower_inv, remainder)
    orbitals = jnp.concatenate([first_q, second_q], axis=0)
    orbitals = lax.dynamic_slice_in_dim(orbitals, lax.axis_index("orb") * orb_rows, orb_rows, 0)
    return (orbitals.reshape(orbital_block.shape), triangle)


def solution(mesh):
    in_specs = (P("orb", "grid", None, None), P("grid", None, None))
    out_specs = (P("orb", "grid", None, None), P())
    return jax.shard_map(local, mesh=mesh, in_specs=in_specs, out_specs=out_specs, check_vma=False)
```

```python
import jax
import jax.numpy as jnp
from jax import lax
from jax.experimental import pallas as pl
from jax.experimental.pallas import tpu as pltpu
from jax.sharding import PartitionSpec as P

coefs = (
    -5369.0 / 1800.0,
    12.0 / 7.0,
    -15.0 / 56.0,
    10.0 / 189.0,
    -1.0 / 112.0,
    2.0 / 1925.0,
    -1.0 / 16632.0,
)
centre = 23.5
radius = 19.5
highest = lax.Precision.HIGHEST


def padded_2(value, sides, width):
    for axis, dim in sides:
        size, length = (lax.axis_size(axis), value.shape[dim])
        up = [(i, (i + 1) % size) for i in range(size - 1)]
        down = [(j, i) for i, j in up]
        last = lax.slice_in_dim(value, length - width, length, axis=dim)
        first = lax.slice_in_dim(value, 0, width, axis=dim)
        before = lax.ppermute(last, axis, up)
        after = lax.ppermute(first, axis, down)
        value = jnp.concatenate([before, value, after], axis=dim)
    return value


def hamiltonian(orbital_field, potential):
    slab_cells = orbital_field.shape[1]
    across = orbital_field.shape[2]
    depth_cells = orbital_field.shape[3]
    widened = padded_2(orbital_field, (("grid", 1),), 6)
    padded = jnp.pad(orbital_field, ((0, 0), (0, 0), (6, 6), (6, 6)))
    total = 3.0 * coefs[0] * orbital_field
    for k in range(1, 7):
        total = total + coefs[k] * (
            widened[:, 6 + k : 6 + k + slab_cells] + widened[:, 6 - k : 6 - k + slab_cells]
        )
        total = total + coefs[k] * (
            padded[:, :, 6 + k : 6 + k + across, 6 : 6 + depth_cells]
            + padded[:, :, 6 - k : 6 - k + across, 6 : 6 + depth_cells]
        )
        total = total + coefs[k] * (
            padded[:, :, 6 : 6 + across, 6 + k : 6 + k + depth_cells]
            + padded[:, :, 6 : 6 + across, 6 - k : 6 - k + depth_cells]
        )
    return -2.0 * total + potential[None] * orbital_field


def gram_matrix(left_rows, right_rows):
    return lax.dot_general(
        left_rows,
        right_rows,
        (((1,), (1,)), ((), ())),
        precision=highest,
        preferred_element_type=jnp.float32,
    )


def apply_rows(inverse, source_rows):
    return lax.dot_general(
        inverse,
        source_rows,
        (((0,), (0,)), ((), ())),
        precision=highest,
        preferred_element_type=jnp.float32,
    )


def mix_rows(weights, source_rows):
    return lax.dot_general(
        weights,
        source_rows,
        (((1,), (0,)), ((), ())),
        precision=highest,
        preferred_element_type=jnp.float32,
    )


def exchange_sum(value, axis):
    size = lax.axis_size(axis)
    if size & (size - 1):
        return lax.psum(value, axis)
    step = 1
    while step < size:
        pairs = [(i, i ^ step) for i in range(size)]
        value = value + lax.ppermute(value, axis, pairs)
        step *= 2
    return value


def cell_sum(value):
    return exchange_sum(exchange_sum(value, "grid"), "orb")


def eliminate_kernel(source_ref, result_ref):
    result_ref[...] = source_ref[...]
    rows, width = result_ref.shape
    lanes = lax.broadcasted_iota(jnp.int32, (1, width), 1)
    cols = lax.broadcasted_iota(jnp.int32, (rows, width), 1)
    row_ids = lax.broadcasted_iota(jnp.int32, (rows, 1), 0)

    def column_step(column, carry):
        current = result_ref[pl.ds(column, 1), :]
        pivot_value = jnp.sum(jnp.where(lanes == column, current, 0.0), axis=1, keepdims=True)
        root = jnp.sqrt(pivot_value)
        scaled = jnp.where(lanes >= column, current, 0.0) / root
        whole = result_ref[...]
        below = jnp.sum(jnp.where(cols == column, whole, 0.0), axis=1, keepdims=True) / root
        below = jnp.where(row_ids > column, below, 0.0)
        whole = whole - below * scaled
        result_ref[...] = jnp.where(row_ids == column, scaled, whole)
        return carry

    lax.fori_loop(0, rows, column_step, 0)


def eliminate(matrix, extra):
    source = jnp.concatenate([matrix, extra], axis=1)
    return pl.pallas_call(
        eliminate_kernel,
        out_shape=jax.ShapeDtypeStruct(source.shape, jnp.float32),
    )(source)


def factorize(rows_block, inv_cells):
    panel_rows = rows_block.shape[0] // 2
    leading = cell_sum(gram_matrix(rows_block[:panel_rows], rows_block)) * inv_cells
    eye = jnp.eye(panel_rows, dtype=jnp.float32)
    first = eliminate(leading, eye)
    first_r = first[:, :panel_rows]
    coupling = first[:, panel_rows : 2 * panel_rows]
    first_lower_inv = first[:, 2 * panel_rows :]
    first_q = mix_rows(first_lower_inv, rows_block[:panel_rows])
    remainder = rows_block[panel_rows:] - apply_rows(coupling, first_q)
    trailing = cell_sum(gram_matrix(remainder, remainder)) * inv_cells
    second = eliminate(trailing, eye)
    second_r = second[:, :panel_rows]
    second_lower_inv = second[:, panel_rows:]
    upper_rows = jnp.concatenate([first_r, coupling], axis=1)
    lower_rows = jnp.concatenate(
        [jnp.zeros((second_r.shape[0], panel_rows), jnp.float32), second_r], axis=1
    )
    triangle = jnp.concatenate([upper_rows, lower_rows], axis=0)
    return triangle, first_q, second_lower_inv, remainder


def local(orbital_block, potential):
    orb_rows = orbital_block.shape[0]
    first = (hamiltonian(orbital_block, potential) - centre * orbital_block) / radius
    filtered = 2.0 * (hamiltonian(first, potential) - centre * first) / radius - orbital_block
    filtered = filtered.reshape(orb_rows, -1)
    inv_cells = 1.0 / (lax.axis_size("grid") * filtered.shape[1])
    spread = lax.all_to_all(filtered, "orb", 1, 0, tiled=True)
    triangle, first_q, second_lower_inv, remainder = factorize(spread, inv_cells)
    second_q = mix_rows(second_lower_inv, remainder)
    orbitals = jnp.concatenate([first_q, second_q], axis=0)
    orbitals = lax.all_to_all(orbitals, "orb", 0, 1, tiled=True)
    return (orbitals.reshape(orbital_block.shape), triangle)


def solution(mesh):
    in_specs = (P("orb", "grid", None, None), P("grid", None, None))
    out_specs = (P("orb", "grid", None, None), P())
    return jax.shard_map(local, mesh=mesh, in_specs=in_specs, out_specs=out_specs, check_vma=False)
```

```python
import jax
import jax.numpy as jnp
from jax import lax
from jax.experimental import pallas as pl
from jax.experimental.pallas import tpu as pltpu
from jax.sharding import PartitionSpec as P

coefs = (
    -5369.0 / 1800.0,
    12.0 / 7.0,
    -15.0 / 56.0,
    10.0 / 189.0,
    -1.0 / 112.0,
    2.0 / 1925.0,
    -1.0 / 16632.0,
)
centre = 23.5
radius = 19.5
highest = lax.Precision.HIGHEST


def halo_planes(value, axis, width):
    size, length = (lax.axis_size(axis), value.shape[1])
    up = [(i, (i + 1) % size) for i in range(size - 1)]
    down = [(j, i) for i, j in up]
    last = lax.slice_in_dim(value, length - width, length, axis=1)
    first = lax.slice_in_dim(value, 0, width, axis=1)
    before = lax.ppermute(last, axis, up)
    after = lax.ppermute(first, axis, down)
    return before, after


def local_terms(orbital_field, potential):
    across = orbital_field.shape[2]
    depth_cells = orbital_field.shape[3]
    padded = jnp.pad(orbital_field, ((0, 0), (0, 0), (6, 6), (6, 6)))
    total = 3.0 * coefs[0] * orbital_field
    for k in range(1, 7):
        total = total + coefs[k] * (
            padded[:, :, 6 + k : 6 + k + across, 6 : 6 + depth_cells]
            + padded[:, :, 6 - k : 6 - k + across, 6 : 6 + depth_cells]
        )
        total = total + coefs[k] * (
            padded[:, :, 6 : 6 + across, 6 + k : 6 + k + depth_cells]
            + padded[:, :, 6 : 6 + across, 6 - k : 6 - k + depth_cells]
        )
    return -2.0 * total + potential[None] * orbital_field


def slab_terms(orbital_field, before, after):
    width = before.shape[1]
    planes = (
        [before[:, q] for q in range(width)]
        + [orbital_field[:, q] for q in range(orbital_field.shape[1])]
        + [after[:, q] for q in range(width)]
    )
    rows = []
    for p in range(orbital_field.shape[1]):
        centre_plane = width + p
        acc = coefs[1] * (planes[centre_plane + 1] + planes[centre_plane - 1])
        for k in range(2, 7):
            acc = acc + coefs[k] * (planes[centre_plane + k] + planes[centre_plane - k])
        rows.append(acc)
    return jnp.stack(rows, axis=1)


def hamiltonian(orbital_field, potential):
    before, after = halo_planes(orbital_field, "grid", 6)
    local = local_terms(orbital_field, potential)
    local, before, after = lax.optimization_barrier((local, before, after))
    return local - 2.0 * slab_terms(orbital_field, before, after)


def gram_matrix(left_rows, right_rows):
    return lax.dot_general(
        left_rows,
        right_rows,
        (((1, 2), (1, 2)), ((), ())),
        precision=highest,
        preferred_element_type=jnp.float32,
    )


def apply_rows(inverse, source_rows):
    return lax.dot_general(
        inverse,
        source_rows,
        (((0,), (0,)), ((), ())),
        precision=highest,
        preferred_element_type=jnp.float32,
    )


def mix_rows(weights, source_rows):
    return lax.dot_general(
        weights,
        source_rows,
        (((1,), (0,)), ((), ())),
        precision=highest,
        preferred_element_type=jnp.float32,
    )


def exchange_sum(value, axis):
    size = lax.axis_size(axis)
    if size & (size - 1):
        return lax.psum(value, axis)
    step = 1
    while step < size:
        pairs = [(i, i ^ step) for i in range(size)]
        value = value + lax.ppermute(value, axis, pairs)
        step *= 2
    return value


def cell_sum(value):
    return exchange_sum(exchange_sum(value, "grid"), "orb")


def eliminate_kernel(source_ref, result_ref):
    result_ref[...] = source_ref[...]
    rows, width = result_ref.shape
    lanes = lax.broadcasted_iota(jnp.int32, (1, width), 1)
    cols = lax.broadcasted_iota(jnp.int32, (rows, width), 1)
    row_ids = lax.broadcasted_iota(jnp.int32, (rows, 1), 0)

    def column_step(column, carry):
        current = result_ref[pl.ds(column, 1), :]
        pivot_value = jnp.sum(jnp.where(lanes == column, current, 0.0), axis=1, keepdims=True)
        root = jnp.sqrt(pivot_value)
        scaled = jnp.where(lanes >= column, current, 0.0) / root
        whole = result_ref[...]
        below = jnp.sum(jnp.where(cols == column, whole, 0.0), axis=1, keepdims=True) / root
        below = jnp.where(row_ids > column, below, 0.0)
        whole = whole - below * scaled
        result_ref[...] = jnp.where(row_ids == column, scaled, whole)
        return carry

    lax.fori_loop(0, rows, column_step, 0)


def eliminate(matrix, extra):
    source = jnp.concatenate([matrix, extra], axis=1)
    return pl.pallas_call(
        eliminate_kernel,
        out_shape=jax.ShapeDtypeStruct(source.shape, jnp.float32),
    )(source)


def factorize(rows_block, inv_cells):
    panel_rows = rows_block.shape[0] // 2
    leading = cell_sum(gram_matrix(rows_block[:panel_rows], rows_block)) * inv_cells
    eye = jnp.eye(panel_rows, dtype=jnp.float32)
    first = eliminate(leading, eye)
    first_r = first[:, :panel_rows]
    coupling = first[:, panel_rows : 2 * panel_rows]
    first_lower_inv = first[:, 2 * panel_rows :]
    first_q = mix_rows(first_lower_inv, rows_block[:panel_rows])
    remainder = rows_block[panel_rows:] - apply_rows(coupling, first_q)
    trailing = cell_sum(gram_matrix(remainder, remainder)) * inv_cells
    second = eliminate(trailing, eye)
    second_r = second[:, :panel_rows]
    second_lower_inv = second[:, panel_rows:]
    upper_rows = jnp.concatenate([first_r, coupling], axis=1)
    lower_rows = jnp.concatenate(
        [jnp.zeros((second_r.shape[0], panel_rows), jnp.float32), second_r], axis=1
    )
    triangle = jnp.concatenate([upper_rows, lower_rows], axis=0)
    return triangle, first_q, second_lower_inv, remainder


def local(orbital_block, potential):
    orb_rows = orbital_block.shape[0]
    first = (hamiltonian(orbital_block, potential) - centre * orbital_block) / radius
    filtered = 2.0 * (hamiltonian(first, potential) - centre * first) / radius - orbital_block
    parts = lax.axis_size("orb")
    lanes = orbital_block.shape[3]
    rows_per_part = orbital_block.shape[1] * orbital_block.shape[2] // parts
    filtered = filtered.reshape(orb_rows, parts, rows_per_part, lanes)
    inv_cells = 1.0 / (lax.axis_size("grid") * parts * rows_per_part * lanes)
    spread = lax.all_to_all(filtered, "orb", 1, 0, tiled=True).reshape(-1, rows_per_part, lanes)
    triangle, first_q, second_lower_inv, remainder = factorize(spread, inv_cells)
    second_q = mix_rows(second_lower_inv, remainder)
    orbitals = jnp.concatenate([first_q, second_q], axis=0)
    orbitals = orbitals.reshape(orbitals.shape[0], 1, rows_per_part, lanes)
    orbitals = lax.all_to_all(orbitals, "orb", 0, 1, tiled=True)
    return (orbitals.reshape(orbital_block.shape), triangle)


def solution(mesh):
    in_specs = (P("orb", "grid", None, None), P("grid", None, None))
    out_specs = (P("orb", "grid", None, None), P())
    return jax.shard_map(local, mesh=mesh, in_specs=in_specs, out_specs=out_specs, check_vma=False)
```

```python
import functools

import jax
import jax.numpy as jnp
from jax import lax
from jax.experimental import pallas as pl
from jax.experimental.pallas import tpu as pltpu
from jax.sharding import PartitionSpec as P

coefs = (
    -5369.0 / 1800.0,
    12.0 / 7.0,
    -15.0 / 56.0,
    10.0 / 189.0,
    -1.0 / 112.0,
    2.0 / 1925.0,
    -1.0 / 16632.0,
)
centre = 23.5
radius = 19.5
highest = lax.Precision.HIGHEST


def halo_planes(value, axis, width):
    size, length = (lax.axis_size(axis), value.shape[1])
    up = [(i, (i + 1) % size) for i in range(size - 1)]
    down = [(j, i) for i, j in up]
    last = lax.slice_in_dim(value, length - width, length, axis=1)
    first = lax.slice_in_dim(value, 0, width, axis=1)
    before = lax.ppermute(last, axis, up)
    after = lax.ppermute(first, axis, down)
    return before, after


def local_terms(orbital_field, potential):
    across = orbital_field.shape[2]
    depth_cells = orbital_field.shape[3]
    padded = jnp.pad(orbital_field, ((0, 0), (0, 0), (6, 6), (6, 6)))
    total = 3.0 * coefs[0] * orbital_field
    for k in range(1, 7):
        total = total + coefs[k] * (
            padded[:, :, 6 + k : 6 + k + across, 6 : 6 + depth_cells]
            + padded[:, :, 6 - k : 6 - k + across, 6 : 6 + depth_cells]
        )
        total = total + coefs[k] * (
            padded[:, :, 6 : 6 + across, 6 + k : 6 + k + depth_cells]
            + padded[:, :, 6 : 6 + across, 6 - k : 6 - k + depth_cells]
        )
    return -2.0 * total + potential[None] * orbital_field


def combine_kernel(scale, with_base, *refs):
    if with_base:
        local_ref, own_ref, before_ref, after_ref, base_ref, out_ref = refs
    else:
        local_ref, own_ref, before_ref, after_ref, out_ref = refs
    width = before_ref.shape[1]
    planes_own = own_ref.shape[1]

    def plane(q):
        if q < 0:
            return before_ref[:, width + q]
        if q >= planes_own:
            return after_ref[:, q - planes_own]
        return own_ref[:, q]

    for p in range(planes_own):
        acc = coefs[1] * (plane(p + 1) + plane(p - 1))
        for k in range(2, 7):
            acc = acc + coefs[k] * (plane(p + k) + plane(p - k))
        value = local_ref[:, p] - 2.0 * acc
        value = scale * (value - centre * own_ref[:, p]) / radius
        if with_base:
            value = value - base_ref[:, p]
        out_ref[:, p] = value


def filter_step(local, orbital_field, before, after, scale, base=None):
    rows = orbital_field.shape[0]
    block_rows = 4 if rows % 4 == 0 else 1
    block = (block_rows,) + orbital_field.shape[1:]
    halo_block = (block_rows,) + before.shape[1:]
    spec = pl.BlockSpec(block, lambda i: (i, 0, 0, 0))
    halo_spec = pl.BlockSpec(halo_block, lambda i: (i, 0, 0, 0))
    operands = [local, orbital_field, before, after]
    specs = [spec, spec, halo_spec, halo_spec]
    if base is not None:
        operands.append(base)
        specs.append(spec)
    return pl.pallas_call(
        functools.partial(combine_kernel, scale, base is not None),
        grid=(rows // block_rows,),
        in_specs=specs,
        out_specs=spec,
        out_shape=jax.ShapeDtypeStruct(orbital_field.shape, jnp.float32),
    )(*operands)


def chebyshev_step(orbital_field, potential, scale, base=None):
    before, after = halo_planes(orbital_field, "grid", 6)
    local = local_terms(orbital_field, potential)
    local, before, after = lax.optimization_barrier((local, before, after))
    return filter_step(local, orbital_field, before, after, scale, base)


def gram_matrix(left_rows, right_rows):
    return lax.dot_general(
        left_rows,
        right_rows,
        (((1, 2), (1, 2)), ((), ())),
        precision=highest,
        preferred_element_type=jnp.float32,
    )


def apply_rows(inverse, source_rows):
    return lax.dot_general(
        inverse,
        source_rows,
        (((0,), (0,)), ((), ())),
        precision=highest,
        preferred_element_type=jnp.float32,
    )


def mix_rows(weights, source_rows):
    return lax.dot_general(
        weights,
        source_rows,
        (((1,), (0,)), ((), ())),
        precision=highest,
        preferred_element_type=jnp.float32,
    )


def group_round(value, axis, stride, radix):
    size = lax.axis_size(axis)
    position = (lax.axis_index(axis) // stride) % radix
    received = [value]
    for shift in range(1, radix):
        pairs = []
        for i in range(size):
            p = (i // stride) % radix
            pairs.append((i, i + ((p + shift) % radix - p) * stride))
        received.append(lax.ppermute(value, axis, pairs))
    total = None
    for q in range(radix):
        choice = (position - q) % radix
        term = received[0]
        for shift in range(1, radix):
            term = jnp.where(choice == shift, received[shift], term)
        total = term if total is None else total + term
    return total


def exchange_sum(value, axis):
    size = lax.axis_size(axis)
    if size & (size - 1):
        return lax.psum(value, axis)
    stride = 1
    if size.bit_length() % 2 == 0:
        value = group_round(value, axis, 1, 2)
        stride = 2
    while stride < size:
        value = group_round(value, axis, stride, 4)
        stride *= 4
    return value


def cell_sum(value):
    return exchange_sum(exchange_sum(value, "grid"), "orb")


def eliminate_kernel(source_ref, result_ref):
    result_ref[...] = source_ref[...]
    rows, width = result_ref.shape
    lanes = lax.broadcasted_iota(jnp.int32, (1, width), 1)
    cols = lax.broadcasted_iota(jnp.int32, (rows, width), 1)
    row_ids = lax.broadcasted_iota(jnp.int32, (rows, 1), 0)

    def column_step(column, carry):
        current = result_ref[pl.ds(column, 1), :]
        pivot_value = jnp.sum(jnp.where(lanes == column, current, 0.0), axis=1, keepdims=True)
        root = jnp.sqrt(pivot_value)
        scaled = jnp.where(lanes >= column, current, 0.0) / root
        whole = result_ref[...]
        below = jnp.sum(jnp.where(cols == column, whole, 0.0), axis=1, keepdims=True) / root
        below = jnp.where(row_ids > column, below, 0.0)
        whole = whole - below * scaled
        result_ref[...] = jnp.where(row_ids == column, scaled, whole)
        return carry

    lax.fori_loop(0, rows, column_step, 0)


def eliminate(matrix, extra):
    source = jnp.concatenate([matrix, extra], axis=1)
    return pl.pallas_call(
        eliminate_kernel,
        out_shape=jax.ShapeDtypeStruct(source.shape, jnp.float32),
    )(source)


def factorize(rows_block, inv_cells):
    panel_rows = rows_block.shape[0] // 2
    leading = cell_sum(gram_matrix(rows_block[:panel_rows], rows_block)) * inv_cells
    eye = jnp.eye(panel_rows, dtype=jnp.float32)
    first = eliminate(leading, eye)
    first_r = first[:, :panel_rows]
    coupling = first[:, panel_rows : 2 * panel_rows]
    first_lower_inv = first[:, 2 * panel_rows :]
    first_q = mix_rows(first_lower_inv, rows_block[:panel_rows])
    remainder = rows_block[panel_rows:] - apply_rows(coupling, first_q)
    trailing = cell_sum(gram_matrix(remainder, remainder)) * inv_cells
    second = eliminate(trailing, eye)
    second_r = second[:, :panel_rows]
    second_lower_inv = second[:, panel_rows:]
    upper_rows = jnp.concatenate([first_r, coupling], axis=1)
    lower_rows = jnp.concatenate(
        [jnp.zeros((second_r.shape[0], panel_rows), jnp.float32), second_r], axis=1
    )
    triangle = jnp.concatenate([upper_rows, lower_rows], axis=0)
    return triangle, first_q, second_lower_inv, remainder


def local(orbital_block, potential):
    orb_rows = orbital_block.shape[0]
    first = chebyshev_step(orbital_block, potential, 1.0)
    filtered = chebyshev_step(first, potential, 2.0, orbital_block)
    parts = lax.axis_size("orb")
    lanes = orbital_block.shape[3]
    rows_per_part = orbital_block.shape[1] * orbital_block.shape[2] // parts
    filtered = filtered.reshape(orb_rows, parts, rows_per_part, lanes)
    inv_cells = 1.0 / (lax.axis_size("grid") * parts * rows_per_part * lanes)
    spread = lax.all_to_all(filtered, "orb", 1, 0, tiled=True).reshape(-1, rows_per_part, lanes)
    triangle, first_q, second_lower_inv, remainder = factorize(spread, inv_cells)
    second_q = mix_rows(second_lower_inv, remainder)
    orbitals = jnp.concatenate([first_q, second_q], axis=0)
    orbitals = orbitals.reshape(orbitals.shape[0], 1, rows_per_part, lanes)
    orbitals = lax.all_to_all(orbitals, "orb", 0, 1, tiled=True)
    return (orbitals.reshape(orbital_block.shape), triangle)


def solution(mesh):
    in_specs = (P("orb", "grid", None, None), P("grid", None, None))
    out_specs = (P("orb", "grid", None, None), P())
    return jax.shard_map(local, mesh=mesh, in_specs=in_specs, out_specs=out_specs, check_vma=False)
```

```python
import functools

import jax
import jax.numpy as jnp
from jax import lax
from jax.experimental import pallas as pl
from jax.experimental.pallas import tpu as pltpu
from jax.sharding import PartitionSpec as P

coefs = (
    -5369.0 / 1800.0,
    12.0 / 7.0,
    -15.0 / 56.0,
    10.0 / 189.0,
    -1.0 / 112.0,
    2.0 / 1925.0,
    -1.0 / 16632.0,
)
centre = 23.5
radius = 19.5
highest = lax.Precision.HIGHEST


def halo_planes(value, axis, width):
    size, length = (lax.axis_size(axis), value.shape[1])
    up = [(i, (i + 1) % size) for i in range(size - 1)]
    down = [(j, i) for i, j in up]
    last = lax.slice_in_dim(value, length - width, length, axis=1)
    first = lax.slice_in_dim(value, 0, width, axis=1)
    before = lax.ppermute(last, axis, up)
    after = lax.ppermute(first, axis, down)
    return before, after


def local_terms(orbital_field, potential):
    across = orbital_field.shape[2]
    depth_cells = orbital_field.shape[3]
    padded = jnp.pad(orbital_field, ((0, 0), (0, 0), (6, 6), (6, 6)))
    total = 3.0 * coefs[0] * orbital_field
    for k in range(1, 7):
        total = total + coefs[k] * (
            padded[:, :, 6 + k : 6 + k + across, 6 : 6 + depth_cells]
            + padded[:, :, 6 - k : 6 - k + across, 6 : 6 + depth_cells]
        )
        total = total + coefs[k] * (
            padded[:, :, 6 : 6 + across, 6 + k : 6 + k + depth_cells]
            + padded[:, :, 6 : 6 + across, 6 - k : 6 - k + depth_cells]
        )
    return -2.0 * total + potential[None] * orbital_field


def combine_kernel(scale, with_base, *refs):
    if with_base:
        local_ref, own_ref, before_ref, after_ref, base_ref, out_ref = refs
    else:
        local_ref, own_ref, before_ref, after_ref, out_ref = refs
    width = before_ref.shape[1]
    planes_own = own_ref.shape[1]

    def plane(q):
        if q < 0:
            return before_ref[:, width + q]
        if q >= planes_own:
            return after_ref[:, q - planes_own]
        return own_ref[:, q]

    for p in range(planes_own):
        acc = coefs[1] * (plane(p + 1) + plane(p - 1))
        for k in range(2, 7):
            acc = acc + coefs[k] * (plane(p + k) + plane(p - k))
        value = local_ref[:, p] - 2.0 * acc
        value = scale * (value - centre * own_ref[:, p]) / radius
        if with_base:
            value = value - base_ref[:, p]
        out_ref[:, p] = value


def filter_step(local, orbital_field, before, after, scale, base=None, start=0, count=None, base_start=0):
    count = orbital_field.shape[0] if count is None else count
    block_rows = 4 if count % 4 == 0 and start % 4 == 0 and base_start % 4 == 0 else 1
    offset = start // block_rows
    base_offset = base_start // block_rows
    block = (block_rows,) + orbital_field.shape[1:]
    halo_block = (block_rows,) + before.shape[1:]
    spec = pl.BlockSpec(block, lambda i: (i + offset, 0, 0, 0))
    halo_spec = pl.BlockSpec(halo_block, lambda i: (i + offset, 0, 0, 0))
    operands = [local, orbital_field, before, after]
    specs = [spec, spec, halo_spec, halo_spec]
    if base is not None:
        operands.append(base)
        specs.append(pl.BlockSpec(block, lambda i: (i + base_offset, 0, 0, 0)))
    return pl.pallas_call(
        functools.partial(combine_kernel, scale, base is not None),
        grid=(count // block_rows,),
        in_specs=specs,
        out_specs=pl.BlockSpec(block, lambda i: (i, 0, 0, 0)),
        out_shape=jax.ShapeDtypeStruct((count,) + orbital_field.shape[1:], jnp.float32),
    )(*operands)


def spread_cells(filtered):
    rows = filtered.shape[0]
    parts = lax.axis_size("orb")
    lanes = filtered.shape[3]
    rows_per_part = filtered.shape[1] * filtered.shape[2] // parts
    chunks = filtered.reshape(rows, parts, rows_per_part, lanes)
    return lax.all_to_all(chunks, "orb", 1, 0, tiled=True).reshape(parts, rows, rows_per_part, lanes)


def gram_matrix(left_rows, right_rows):
    return lax.dot_general(
        left_rows,
        right_rows,
        (((1, 2), (1, 2)), ((), ())),
        precision=highest,
        preferred_element_type=jnp.float32,
    )


def apply_rows(inverse, source_rows):
    return lax.dot_general(
        inverse,
        source_rows,
        (((0,), (0,)), ((), ())),
        precision=highest,
        preferred_element_type=jnp.float32,
    )


def mix_rows(weights, source_rows):
    return lax.dot_general(
        weights,
        source_rows,
        (((1,), (0,)), ((), ())),
        precision=highest,
        preferred_element_type=jnp.float32,
    )


def group_round(value, axis, stride, radix):
    size = lax.axis_size(axis)
    position = (lax.axis_index(axis) // stride) % radix
    received = [value]
    for shift in range(1, radix):
        pairs = []
        for i in range(size):
            p = (i // stride) % radix
            pairs.append((i, i + ((p + shift) % radix - p) * stride))
        received.append(lax.ppermute(value, axis, pairs))
    total = None
    for q in range(radix):
        choice = (position - q) % radix
        term = received[0]
        for shift in range(1, radix):
            term = jnp.where(choice == shift, received[shift], term)
        total = term if total is None else total + term
    return total


def exchange_sum(value, axis):
    size = lax.axis_size(axis)
    if size & (size - 1):
        return lax.psum(value, axis)
    stride = 1
    if size.bit_length() % 2 == 0:
        value = group_round(value, axis, 1, 2)
        stride = 2
    while stride < size:
        value = group_round(value, axis, stride, 4)
        stride *= 4
    return value


def cell_sum(value):
    return exchange_sum(exchange_sum(value, "grid"), "orb")


def eliminate_kernel(source_ref, result_ref):
    result_ref[...] = source_ref[...]
    rows, width = result_ref.shape
    lanes = lax.broadcasted_iota(jnp.int32, (1, width), 1)
    cols = lax.broadcasted_iota(jnp.int32, (rows, width), 1)
    row_ids = lax.broadcasted_iota(jnp.int32, (rows, 1), 0)

    def column_step(column, carry):
        current = result_ref[pl.ds(column, 1), :]
        pivot_value = jnp.sum(jnp.where(lanes == column, current, 0.0), axis=1, keepdims=True)
        root = jnp.sqrt(pivot_value)
        scaled = jnp.where(lanes >= column, current, 0.0) / root
        whole = result_ref[...]
        below = jnp.sum(jnp.where(cols == column, whole, 0.0), axis=1, keepdims=True) / root
        below = jnp.where(row_ids > column, below, 0.0)
        whole = whole - below * scaled
        result_ref[...] = jnp.where(row_ids == column, scaled, whole)
        return carry

    lax.fori_loop(0, rows, column_step, 0)


def eliminate(matrix, extra):
    source = jnp.concatenate([matrix, extra], axis=1)
    return pl.pallas_call(
        eliminate_kernel,
        out_shape=jax.ShapeDtypeStruct(source.shape, jnp.float32),
    )(source)


def factorize(rows_block, inv_cells):
    panel_rows = rows_block.shape[0] // 2
    leading = cell_sum(gram_matrix(rows_block[:panel_rows], rows_block)) * inv_cells
    eye = jnp.eye(panel_rows, dtype=jnp.float32)
    first = eliminate(leading, eye)
    first_r = first[:, :panel_rows]
    coupling = first[:, panel_rows : 2 * panel_rows]
    first_lower_inv = first[:, 2 * panel_rows :]
    first_q = mix_rows(first_lower_inv, rows_block[:panel_rows])
    remainder = rows_block[panel_rows:] - apply_rows(coupling, first_q)
    trailing = cell_sum(gram_matrix(remainder, remainder)) * inv_cells
    second = eliminate(trailing, eye)
    second_r = second[:, :panel_rows]
    second_lower_inv = second[:, panel_rows:]
    upper_rows = jnp.concatenate([first_r, coupling], axis=1)
    lower_rows = jnp.concatenate(
        [jnp.zeros((second_r.shape[0], panel_rows), jnp.float32), second_r], axis=1
    )
    triangle = jnp.concatenate([upper_rows, lower_rows], axis=0)
    return triangle, first_q, second_lower_inv, remainder


def local(orbital_block, potential):
    orb_rows = orbital_block.shape[0]
    half = orb_rows // 2
    before, after = halo_planes(orbital_block, "grid", 6)
    local_part = local_terms(orbital_block, potential)
    local_part, before, after = lax.optimization_barrier((local_part, before, after))
    first_a = filter_step(local_part, orbital_block, before, after, 1.0, start=0, count=half)
    first_b = filter_step(local_part, orbital_block, before, after, 1.0, start=half, count=orb_rows - half)
    before_a, after_a = halo_planes(first_a, "grid", 6)
    local_a = local_terms(first_a, potential)
    local_a, before_a, after_a, first_b = lax.optimization_barrier((local_a, before_a, after_a, first_b))
    before_b, after_b = halo_planes(first_b, "grid", 6)
    filtered_a = filter_step(local_a, first_a, before_a, after_a, 2.0, base=orbital_block)
    spread_a = spread_cells(filtered_a)
    local_b = local_terms(first_b, potential)
    local_b, before_b, after_b = lax.optimization_barrier((local_b, before_b, after_b))
    filtered_b = lax.optimization_barrier(
        filter_step(local_b, first_b, before_b, after_b, 2.0, base=orbital_block, base_start=half)
    )
    spread_b = spread_cells(filtered_b)
    parts, _, rows_per_part, lanes = spread_a.shape
    spread = jnp.stack([spread_a, spread_b], axis=1).reshape(-1, rows_per_part, lanes)
    inv_cells = 1.0 / (lax.axis_size("grid") * parts * rows_per_part * lanes)
    triangle, first_q, second_lower_inv, remainder = factorize(spread, inv_cells)
    second_q = mix_rows(second_lower_inv, remainder)
    orbitals = jnp.concatenate([first_q, second_q], axis=0)
    orbitals = orbitals.reshape(orbitals.shape[0], 1, rows_per_part, lanes)
    orbitals = lax.all_to_all(orbitals, "orb", 0, 1, tiled=True)
    return (orbitals.reshape(orbital_block.shape), triangle)


def solution(mesh):
    in_specs = (P("orb", "grid", None, None), P("grid", None, None))
    out_specs = (P("orb", "grid", None, None), P())
    return jax.shard_map(local, mesh=mesh, in_specs=in_specs, out_specs=out_specs, check_vma=False)
```

```python
import functools

import jax
import jax.numpy as jnp
from jax import lax
from jax.experimental import pallas as pl
from jax.experimental.pallas import tpu as pltpu
from jax.sharding import PartitionSpec as P

coefs = (
    -5369.0 / 1800.0,
    12.0 / 7.0,
    -15.0 / 56.0,
    10.0 / 189.0,
    -1.0 / 112.0,
    2.0 / 1925.0,
    -1.0 / 16632.0,
)
centre = 23.5
radius = 19.5
highest = lax.Precision.HIGHEST


def halo_planes(value, axis, width):
    size, length = (lax.axis_size(axis), value.shape[1])
    up = [(i, (i + 1) % size) for i in range(size - 1)]
    down = [(j, i) for i, j in up]
    last = lax.slice_in_dim(value, length - width, length, axis=1)
    first = lax.slice_in_dim(value, 0, width, axis=1)
    before = lax.ppermute(last, axis, up)
    after = lax.ppermute(first, axis, down)
    return before, after


def local_terms(orbital_field, potential):
    across = orbital_field.shape[2]
    depth_cells = orbital_field.shape[3]
    padded = jnp.pad(orbital_field, ((0, 0), (0, 0), (6, 6), (6, 6)))
    total = 3.0 * coefs[0] * orbital_field
    for k in range(1, 7):
        total = total + coefs[k] * (
            padded[:, :, 6 + k : 6 + k + across, 6 : 6 + depth_cells]
            + padded[:, :, 6 - k : 6 - k + across, 6 : 6 + depth_cells]
        )
        total = total + coefs[k] * (
            padded[:, :, 6 : 6 + across, 6 + k : 6 + k + depth_cells]
            + padded[:, :, 6 : 6 + across, 6 - k : 6 - k + depth_cells]
        )
    return -2.0 * total + potential[None] * orbital_field


def combine_kernel(scale, with_base, *refs):
    if with_base:
        local_ref, own_ref, before_ref, after_ref, base_ref, out_ref = refs
    else:
        local_ref, own_ref, before_ref, after_ref, out_ref = refs
    width = before_ref.shape[1]
    planes_own = own_ref.shape[1]

    def plane(q):
        if q < 0:
            return before_ref[:, width + q]
        if q >= planes_own:
            return after_ref[:, q - planes_own]
        return own_ref[:, q]

    for p in range(planes_own):
        acc = coefs[1] * (plane(p + 1) + plane(p - 1))
        for k in range(2, 7):
            acc = acc + coefs[k] * (plane(p + k) + plane(p - k))
        value = local_ref[:, p] - 2.0 * acc
        value = scale * (value - centre * own_ref[:, p]) / radius
        if with_base:
            value = value - base_ref[:, p]
        out_ref[:, p] = value


def filter_step(local, orbital_field, before, after, scale, base=None, start=0, count=None, base_start=0):
    count = orbital_field.shape[0] if count is None else count
    block_rows = 4 if count % 4 == 0 and start % 4 == 0 and base_start % 4 == 0 else 1
    offset = start // block_rows
    base_offset = base_start // block_rows
    block = (block_rows,) + orbital_field.shape[1:]
    halo_block = (block_rows,) + before.shape[1:]
    spec = pl.BlockSpec(block, lambda i: (i + offset, 0, 0, 0))
    halo_spec = pl.BlockSpec(halo_block, lambda i: (i + offset, 0, 0, 0))
    operands = [local, orbital_field, before, after]
    specs = [spec, spec, halo_spec, halo_spec]
    if base is not None:
        operands.append(base)
        specs.append(pl.BlockSpec(block, lambda i: (i + base_offset, 0, 0, 0)))
    return pl.pallas_call(
        functools.partial(combine_kernel, scale, base is not None),
        grid=(count // block_rows,),
        in_specs=specs,
        out_specs=pl.BlockSpec(block, lambda i: (i, 0, 0, 0)),
        out_shape=jax.ShapeDtypeStruct((count,) + orbital_field.shape[1:], jnp.float32),
    )(*operands)


def spread_cells(filtered):
    rows = filtered.shape[0]
    parts = lax.axis_size("orb")
    lanes = filtered.shape[3]
    rows_per_part = filtered.shape[1] * filtered.shape[2] // parts
    chunks = filtered.reshape(rows, parts, rows_per_part, lanes)
    return lax.all_to_all(chunks, "orb", 1, 0, tiled=True).reshape(parts, rows, rows_per_part, lanes)


def gram_matrix(left_rows, right_rows):
    return lax.dot_general(
        left_rows,
        right_rows,
        (((1, 2), (1, 2)), ((), ())),
        precision=highest,
        preferred_element_type=jnp.float32,
    )


def apply_rows(inverse, source_rows):
    return lax.dot_general(
        inverse,
        source_rows,
        (((0,), (0,)), ((), ())),
        precision=highest,
        preferred_element_type=jnp.float32,
    )


def mix_rows(weights, source_rows):
    return lax.dot_general(
        weights,
        source_rows,
        (((1,), (0,)), ((), ())),
        precision=highest,
        preferred_element_type=jnp.float32,
    )


def group_round(value, axis, stride, radix):
    size = lax.axis_size(axis)
    position = (lax.axis_index(axis) // stride) % radix
    received = [value]
    for shift in range(1, radix):
        pairs = []
        for i in range(size):
            p = (i // stride) % radix
            pairs.append((i, i + ((p + shift) % radix - p) * stride))
        received.append(lax.ppermute(value, axis, pairs))
    total = None
    for q in range(radix):
        choice = (position - q) % radix
        term = received[0]
        for shift in range(1, radix):
            term = jnp.where(choice == shift, received[shift], term)
        total = term if total is None else total + term
    return total


def exchange_sum(value, axis):
    size = lax.axis_size(axis)
    if size & (size - 1):
        return lax.psum(value, axis)
    stride = 1
    if size.bit_length() % 2 == 0:
        value = group_round(value, axis, 1, 2)
        stride = 2
    while stride < size:
        value = group_round(value, axis, stride, 4)
        stride *= 4
    return value


def cell_sum(value):
    return exchange_sum(exchange_sum(value, "grid"), "orb")


def eliminate_kernel(source_ref, result_ref):
    rows, width = result_ref.shape
    lanes = lax.broadcasted_iota(jnp.int32, (1, width), 1)
    cols = lax.broadcasted_iota(jnp.int32, (rows, width), 1)
    row_ids = lax.broadcasted_iota(jnp.int32, (rows, 1), 0)

    def column_step(column, whole):
        current = jnp.sum(jnp.where(row_ids == column, whole, 0.0), axis=0, keepdims=True)
        pivot_value = jnp.sum(jnp.where(lanes == column, current, 0.0), axis=1, keepdims=True)
        root = jnp.sqrt(pivot_value)
        scaled = jnp.where(lanes >= column, current, 0.0) / root
        below = jnp.sum(jnp.where(cols == column, whole, 0.0), axis=1, keepdims=True) / root
        below = jnp.where(row_ids > column, below, 0.0)
        whole = whole - below * scaled
        return jnp.where(row_ids == column, scaled, whole)

    result_ref[...] = lax.fori_loop(0, rows, column_step, source_ref[...], unroll=4)


def eliminate(matrix, extra):
    source = jnp.concatenate([matrix, extra], axis=1)
    return pl.pallas_call(
        eliminate_kernel,
        out_shape=jax.ShapeDtypeStruct(source.shape, jnp.float32),
    )(source)


def factorize(rows_block, inv_cells):
    panel_rows = rows_block.shape[0] // 2
    leading = cell_sum(gram_matrix(rows_block[:panel_rows], rows_block)) * inv_cells
    eye = jnp.eye(panel_rows, dtype=jnp.float32)
    first = eliminate(leading, eye)
    first_r = first[:, :panel_rows]
    coupling = first[:, panel_rows : 2 * panel_rows]
    first_lower_inv = first[:, 2 * panel_rows :]
    first_q = mix_rows(first_lower_inv, rows_block[:panel_rows])
    remainder = rows_block[panel_rows:] - apply_rows(coupling, first_q)
    trailing = cell_sum(gram_matrix(remainder, remainder)) * inv_cells
    second = eliminate(trailing, eye)
    second_r = second[:, :panel_rows]
    second_lower_inv = second[:, panel_rows:]
    upper_rows = jnp.concatenate([first_r, coupling], axis=1)
    lower_rows = jnp.concatenate(
        [jnp.zeros((second_r.shape[0], panel_rows), jnp.float32), second_r], axis=1
    )
    triangle = jnp.concatenate([upper_rows, lower_rows], axis=0)
    return triangle, first_q, second_lower_inv, remainder


def local(orbital_block, potential):
    orb_rows = orbital_block.shape[0]
    half = orb_rows // 2
    before, after = halo_planes(orbital_block, "grid", 6)
    local_part = local_terms(orbital_block, potential)
    local_part, before, after = lax.optimization_barrier((local_part, before, after))
    first_a = filter_step(local_part, orbital_block, before, after, 1.0, start=0, count=half)
    first_b = filter_step(local_part, orbital_block, before, after, 1.0, start=half, count=orb_rows - half)
    before_a, after_a = halo_planes(first_a, "grid", 6)
    local_a = local_terms(first_a, potential)
    local_a, before_a, after_a, first_b = lax.optimization_barrier((local_a, before_a, after_a, first_b))
    before_b, after_b = halo_planes(first_b, "grid", 6)
    filtered_a = filter_step(local_a, first_a, before_a, after_a, 2.0, base=orbital_block)
    spread_a = spread_cells(filtered_a)
    local_b = local_terms(first_b, potential)
    local_b, before_b, after_b = lax.optimization_barrier((local_b, before_b, after_b))
    filtered_b = lax.optimization_barrier(
        filter_step(local_b, first_b, before_b, after_b, 2.0, base=orbital_block, base_start=half)
    )
    spread_b = spread_cells(filtered_b)
    parts, _, rows_per_part, lanes = spread_a.shape
    spread = jnp.stack([spread_a, spread_b], axis=1).reshape(-1, rows_per_part, lanes)
    inv_cells = 1.0 / (lax.axis_size("grid") * parts * rows_per_part * lanes)
    triangle, first_q, second_lower_inv, remainder = factorize(spread, inv_cells)
    second_q = mix_rows(second_lower_inv, remainder)
    orbitals = jnp.concatenate([first_q, second_q], axis=0)
    orbitals = orbitals.reshape(orbitals.shape[0], 1, rows_per_part, lanes)
    orbitals = lax.all_to_all(orbitals, "orb", 0, 1, tiled=True)
    return (orbitals.reshape(orbital_block.shape), triangle)


def solution(mesh):
    in_specs = (P("orb", "grid", None, None), P("grid", None, None))
    out_specs = (P("orb", "grid", None, None), P())
    return jax.shard_map(local, mesh=mesh, in_specs=in_specs, out_specs=out_specs, check_vma=False)
```

```python
import functools

import jax
import jax.numpy as jnp
from jax import lax
from jax.experimental import pallas as pl
from jax.experimental.pallas import tpu as pltpu
from jax.sharding import PartitionSpec as P

coefs = (
    -5369.0 / 1800.0,
    12.0 / 7.0,
    -15.0 / 56.0,
    10.0 / 189.0,
    -1.0 / 112.0,
    2.0 / 1925.0,
    -1.0 / 16632.0,
)
centre = 23.5
radius = 19.5
highest = lax.Precision.HIGHEST


def halo_planes(value, axis, width):
    size, length = (lax.axis_size(axis), value.shape[1])
    up = [(i, (i + 1) % size) for i in range(size - 1)]
    down = [(j, i) for i, j in up]
    last = lax.slice_in_dim(value, length - width, length, axis=1)
    first = lax.slice_in_dim(value, 0, width, axis=1)
    before = lax.ppermute(last, axis, up)
    after = lax.ppermute(first, axis, down)
    return before, after


def local_terms(orbital_field, potential):
    across = orbital_field.shape[2]
    depth_cells = orbital_field.shape[3]
    padded = jnp.pad(orbital_field, ((0, 0), (0, 0), (6, 6), (6, 6)))
    total = 3.0 * coefs[0] * orbital_field
    for k in range(1, 7):
        total = total + coefs[k] * (
            padded[:, :, 6 + k : 6 + k + across, 6 : 6 + depth_cells]
            + padded[:, :, 6 - k : 6 - k + across, 6 : 6 + depth_cells]
        )
        total = total + coefs[k] * (
            padded[:, :, 6 : 6 + across, 6 + k : 6 + k + depth_cells]
            + padded[:, :, 6 : 6 + across, 6 - k : 6 - k + depth_cells]
        )
    return -2.0 * total + potential[None] * orbital_field


def combine_kernel(scale, with_base, *refs):
    if with_base:
        local_ref, own_ref, before_ref, after_ref, base_ref, out_ref = refs
    else:
        local_ref, own_ref, before_ref, after_ref, out_ref = refs
    width = before_ref.shape[1]
    planes_own = own_ref.shape[1]

    def plane(q):
        if q < 0:
            return before_ref[:, width + q]
        if q >= planes_own:
            return after_ref[:, q - planes_own]
        return own_ref[:, q]

    for p in range(planes_own):
        acc = coefs[1] * (plane(p + 1) + plane(p - 1))
        for k in range(2, 7):
            acc = acc + coefs[k] * (plane(p + k) + plane(p - k))
        value = local_ref[:, p] - 2.0 * acc
        value = scale * (value - centre * own_ref[:, p]) / radius
        if with_base:
            value = value - base_ref[:, p]
        out_ref[:, p] = value


def filter_step(local, orbital_field, before, after, scale, base=None, start=0, count=None, base_start=0):
    count = orbital_field.shape[0] if count is None else count
    block_rows = 4 if count % 4 == 0 and start % 4 == 0 and base_start % 4 == 0 else 1
    offset = start // block_rows
    base_offset = base_start // block_rows
    block = (block_rows,) + orbital_field.shape[1:]
    halo_block = (block_rows,) + before.shape[1:]
    spec = pl.BlockSpec(block, lambda i: (i + offset, 0, 0, 0))
    halo_spec = pl.BlockSpec(halo_block, lambda i: (i + offset, 0, 0, 0))
    operands = [local, orbital_field, before, after]
    specs = [spec, spec, halo_spec, halo_spec]
    if base is not None:
        operands.append(base)
        specs.append(pl.BlockSpec(block, lambda i: (i + base_offset, 0, 0, 0)))
    return pl.pallas_call(
        functools.partial(combine_kernel, scale, base is not None),
        grid=(count // block_rows,),
        in_specs=specs,
        out_specs=pl.BlockSpec(block, lambda i: (i, 0, 0, 0)),
        out_shape=jax.ShapeDtypeStruct((count,) + orbital_field.shape[1:], jnp.float32),
    )(*operands)


def spread_cells(filtered):
    rows = filtered.shape[0]
    parts = lax.axis_size("orb")
    lanes = filtered.shape[3]
    rows_per_part = filtered.shape[1] * filtered.shape[2] // parts
    chunks = filtered.reshape(rows, parts, rows_per_part, lanes)
    return lax.all_to_all(chunks, "orb", 1, 0, tiled=True).reshape(parts, rows, rows_per_part, lanes)


def gram_matrix(left_rows, right_rows):
    return lax.dot_general(
        left_rows,
        right_rows,
        (((1, 2), (1, 2)), ((), ())),
        precision=highest,
        preferred_element_type=jnp.float32,
    )


def apply_rows(inverse, source_rows):
    return lax.dot_general(
        inverse,
        source_rows,
        (((0,), (0,)), ((), ())),
        precision=highest,
        preferred_element_type=jnp.float32,
    )


def mix_rows(weights, source_rows):
    return lax.dot_general(
        weights,
        source_rows,
        (((1,), (0,)), ((), ())),
        precision=highest,
        preferred_element_type=jnp.float32,
    )


def group_round(value, axis, stride, radix):
    size = lax.axis_size(axis)
    position = (lax.axis_index(axis) // stride) % radix
    received = [value]
    for shift in range(1, radix):
        pairs = []
        for i in range(size):
            p = (i // stride) % radix
            pairs.append((i, i + ((p + shift) % radix - p) * stride))
        received.append(lax.ppermute(value, axis, pairs))
    total = None
    for q in range(radix):
        choice = (position - q) % radix
        term = received[0]
        for shift in range(1, radix):
            term = jnp.where(choice == shift, received[shift], term)
        total = term if total is None else total + term
    return total


def exchange_sum(value, axis):
    size = lax.axis_size(axis)
    if size & (size - 1):
        return lax.psum(value, axis)
    stride = 1
    if size.bit_length() % 2 == 0:
        value = group_round(value, axis, 1, 2)
        stride = 2
    while stride < size:
        value = group_round(value, axis, stride, 4)
        stride *= 4
    return value


def cell_sum(value):
    return exchange_sum(exchange_sum(value, "grid"), "orb")


def eliminate_kernel(source_ref, result_ref):
    result_ref[...] = source_ref[...]
    rows, width = result_ref.shape
    lanes = lax.broadcasted_iota(jnp.int32, (1, width), 1)
    cols = lax.broadcasted_iota(jnp.int32, (rows, width), 1)
    row_ids = lax.broadcasted_iota(jnp.int32, (rows, 1), 0)

    def column_step(column, carry):
        current = result_ref[pl.ds(column, 1), :]
        pivot_value = jnp.sum(jnp.where(lanes == column, current, 0.0), axis=1, keepdims=True)
        root = jnp.sqrt(pivot_value)
        scaled = jnp.where(lanes >= column, current, 0.0) / root
        whole = result_ref[...]
        below = jnp.sum(jnp.where(cols == column, whole, 0.0), axis=1, keepdims=True) / root
        below = jnp.where(row_ids > column, below, 0.0)
        whole = whole - below * scaled
        result_ref[...] = jnp.where(row_ids == column, scaled, whole)
        return carry

    lax.fori_loop(0, rows, column_step, 0)


def eliminate(matrix, extra):
    source = jnp.concatenate([matrix, extra], axis=1)
    return pl.pallas_call(
        eliminate_kernel,
        out_shape=jax.ShapeDtypeStruct(source.shape, jnp.float32),
    )(source)


def factorize(rows_block, inv_cells):
    panel_rows = rows_block.shape[0] // 2
    leading = cell_sum(gram_matrix(rows_block[:panel_rows], rows_block)) * inv_cells
    eye = jnp.eye(panel_rows, dtype=jnp.float32)
    first = eliminate(leading, eye)
    first_r = first[:, :panel_rows]
    coupling = first[:, panel_rows : 2 * panel_rows]
    first_lower_inv = first[:, 2 * panel_rows :]
    first_q = mix_rows(first_lower_inv, rows_block[:panel_rows])
    remainder = rows_block[panel_rows:] - apply_rows(coupling, first_q)
    trailing = cell_sum(gram_matrix(remainder, remainder)) * inv_cells
    second = eliminate(trailing, eye)
    second_r = second[:, :panel_rows]
    second_lower_inv = second[:, panel_rows:]
    upper_rows = jnp.concatenate([first_r, coupling], axis=1)
    lower_rows = jnp.concatenate(
        [jnp.zeros((second_r.shape[0], panel_rows), jnp.float32), second_r], axis=1
    )
    triangle = jnp.concatenate([upper_rows, lower_rows], axis=0)
    coupled = mix_rows(second_lower_inv, apply_rows(coupling, first_lower_inv))
    lower_inverse = jnp.concatenate(
        [
            jnp.concatenate([first_lower_inv, jnp.zeros_like(first_lower_inv)], axis=1),
            jnp.concatenate([-coupled, second_lower_inv], axis=1),
        ],
        axis=0,
    )
    return triangle, mix_rows(lower_inverse, rows_block)


def local(orbital_block, potential):
    orb_rows = orbital_block.shape[0]
    half = orb_rows // 2
    before, after = halo_planes(orbital_block, "grid", 6)
    local_part = local_terms(orbital_block, potential)
    local_part, before, after = lax.optimization_barrier((local_part, before, after))
    first_a = filter_step(local_part, orbital_block, before, after, 1.0, start=0, count=half)
    first_b = filter_step(local_part, orbital_block, before, after, 1.0, start=half, count=orb_rows - half)
    before_a, after_a = halo_planes(first_a, "grid", 6)
    local_a = local_terms(first_a, potential)
    local_a, before_a, after_a, first_b = lax.optimization_barrier((local_a, before_a, after_a, first_b))
    before_b, after_b = halo_planes(first_b, "grid", 6)
    filtered_a = filter_step(local_a, first_a, before_a, after_a, 2.0, base=orbital_block)
    spread_a = spread_cells(filtered_a)
    local_b = local_terms(first_b, potential)
    local_b, before_b, after_b = lax.optimization_barrier((local_b, before_b, after_b))
    filtered_b = lax.optimization_barrier(
        filter_step(local_b, first_b, before_b, after_b, 2.0, base=orbital_block, base_start=half)
    )
    spread_b = spread_cells(filtered_b)
    parts, _, rows_per_part, lanes = spread_a.shape
    spread = jnp.stack([spread_a, spread_b], axis=1).reshape(-1, rows_per_part, lanes)
    inv_cells = 1.0 / (lax.axis_size("grid") * parts * rows_per_part * lanes)
    triangle, orbitals = factorize(spread, inv_cells)
    orbitals = orbitals.reshape(orbitals.shape[0], 1, rows_per_part, lanes)
    orbitals = lax.all_to_all(orbitals, "orb", 0, 1, tiled=True)
    return (orbitals.reshape(orbital_block.shape), triangle)


def solution(mesh):
    in_specs = (P("orb", "grid", None, None), P("grid", None, None))
    out_specs = (P("orb", "grid", None, None), P())
    return jax.shard_map(local, mesh=mesh, in_specs=in_specs, out_specs=out_specs, check_vma=False)
```

```python
import functools

import jax
import jax.numpy as jnp
from jax import lax
from jax.experimental import pallas as pl
from jax.experimental.pallas import tpu as pltpu
from jax.sharding import PartitionSpec as P

coefs = (
    -5369.0 / 1800.0,
    12.0 / 7.0,
    -15.0 / 56.0,
    10.0 / 189.0,
    -1.0 / 112.0,
    2.0 / 1925.0,
    -1.0 / 16632.0,
)
centre = 23.5
radius = 19.5
matmul_precision = lax.Precision.HIGH


def halo_planes(value, axis, width):
    size, length = (lax.axis_size(axis), value.shape[1])
    up = [(i, (i + 1) % size) for i in range(size - 1)]
    down = [(j, i) for i, j in up]
    last = lax.slice_in_dim(value, length - width, length, axis=1)
    first = lax.slice_in_dim(value, 0, width, axis=1)
    before = lax.ppermute(last, axis, up)
    after = lax.ppermute(first, axis, down)
    return before, after


def local_terms(orbital_field, potential):
    across = orbital_field.shape[2]
    depth_cells = orbital_field.shape[3]
    padded = jnp.pad(orbital_field, ((0, 0), (0, 0), (6, 6), (6, 6)))
    total = 3.0 * coefs[0] * orbital_field
    for k in range(1, 7):
        total = total + coefs[k] * (
            padded[:, :, 6 + k : 6 + k + across, 6 : 6 + depth_cells]
            + padded[:, :, 6 - k : 6 - k + across, 6 : 6 + depth_cells]
        )
        total = total + coefs[k] * (
            padded[:, :, 6 : 6 + across, 6 + k : 6 + k + depth_cells]
            + padded[:, :, 6 : 6 + across, 6 - k : 6 - k + depth_cells]
        )
    return -2.0 * total + potential[None] * orbital_field


def combine_kernel(scale, with_base, *refs):
    if with_base:
        local_ref, own_ref, before_ref, after_ref, base_ref, out_ref = refs
    else:
        local_ref, own_ref, before_ref, after_ref, out_ref = refs
    width = before_ref.shape[1]
    planes_own = own_ref.shape[1]

    def plane(q):
        if q < 0:
            return before_ref[:, width + q]
        if q >= planes_own:
            return after_ref[:, q - planes_own]
        return own_ref[:, q]

    for p in range(planes_own):
        acc = coefs[1] * (plane(p + 1) + plane(p - 1))
        for k in range(2, 7):
            acc = acc + coefs[k] * (plane(p + k) + plane(p - k))
        value = local_ref[:, p] - 2.0 * acc
        value = scale * (value - centre * own_ref[:, p]) / radius
        if with_base:
            value = value - base_ref[:, p]
        out_ref[:, p] = value


def filter_step(local, orbital_field, before, after, scale, base=None, start=0, count=None, base_start=0):
    count = orbital_field.shape[0] if count is None else count
    block_rows = 4 if count % 4 == 0 and start % 4 == 0 and base_start % 4 == 0 else 1
    offset = start // block_rows
    base_offset = base_start // block_rows
    block = (block_rows,) + orbital_field.shape[1:]
    halo_block = (block_rows,) + before.shape[1:]
    spec = pl.BlockSpec(block, lambda i: (i + offset, 0, 0, 0))
    halo_spec = pl.BlockSpec(halo_block, lambda i: (i + offset, 0, 0, 0))
    operands = [local, orbital_field, before, after]
    specs = [spec, spec, halo_spec, halo_spec]
    if base is not None:
        operands.append(base)
        specs.append(pl.BlockSpec(block, lambda i: (i + base_offset, 0, 0, 0)))
    return pl.pallas_call(
        functools.partial(combine_kernel, scale, base is not None),
        grid=(count // block_rows,),
        in_specs=specs,
        out_specs=pl.BlockSpec(block, lambda i: (i, 0, 0, 0)),
        out_shape=jax.ShapeDtypeStruct((count,) + orbital_field.shape[1:], jnp.float32),
    )(*operands)


def spread_cells(filtered):
    rows = filtered.shape[0]
    parts = lax.axis_size("orb")
    lanes = filtered.shape[3]
    rows_per_part = filtered.shape[1] * filtered.shape[2] // parts
    chunks = filtered.reshape(rows, parts, rows_per_part, lanes)
    return lax.all_to_all(chunks, "orb", 1, 0, tiled=True).reshape(parts, rows, rows_per_part, lanes)


def gram_matrix(left_rows, right_rows):
    return lax.dot_general(
        left_rows,
        right_rows,
        (((1, 2), (1, 2)), ((), ())),
        precision=matmul_precision,
        preferred_element_type=jnp.float32,
    )


def apply_rows(inverse, source_rows):
    return lax.dot_general(
        inverse,
        source_rows,
        (((0,), (0,)), ((), ())),
        precision=matmul_precision,
        preferred_element_type=jnp.float32,
    )


def mix_rows(weights, source_rows):
    return lax.dot_general(
        weights,
        source_rows,
        (((1,), (0,)), ((), ())),
        precision=matmul_precision,
        preferred_element_type=jnp.float32,
    )


def group_round(value, axis, stride, radix):
    size = lax.axis_size(axis)
    position = (lax.axis_index(axis) // stride) % radix
    received = [value]
    for shift in range(1, radix):
        pairs = []
        for i in range(size):
            p = (i // stride) % radix
            pairs.append((i, i + ((p + shift) % radix - p) * stride))
        received.append(lax.ppermute(value, axis, pairs))
    total = None
    for q in range(radix):
        choice = (position - q) % radix
        term = received[0]
        for shift in range(1, radix):
            term = jnp.where(choice == shift, received[shift], term)
        total = term if total is None else total + term
    return total


def exchange_sum(value, axis):
    size = lax.axis_size(axis)
    if size & (size - 1):
        return lax.psum(value, axis)
    stride = 1
    if size.bit_length() % 2 == 0:
        value = group_round(value, axis, 1, 2)
        stride = 2
    while stride < size:
        value = group_round(value, axis, stride, 4)
        stride *= 4
    return value


def cell_sum(value):
    return exchange_sum(exchange_sum(value, "grid"), "orb")


def eliminate_kernel(source_ref, result_ref):
    result_ref[...] = source_ref[...]
    rows, width = result_ref.shape
    lanes = lax.broadcasted_iota(jnp.int32, (1, width), 1)
    cols = lax.broadcasted_iota(jnp.int32, (rows, width), 1)
    row_ids = lax.broadcasted_iota(jnp.int32, (rows, 1), 0)

    def column_step(column, carry):
        current = result_ref[pl.ds(column, 1), :]
        pivot_value = jnp.sum(jnp.where(lanes == column, current, 0.0), axis=1, keepdims=True)
        root = jnp.sqrt(pivot_value)
        scaled = jnp.where(lanes >= column, current, 0.0) / root
        whole = result_ref[...]
        below = jnp.sum(jnp.where(cols == column, whole, 0.0), axis=1, keepdims=True) / root
        below = jnp.where(row_ids > column, below, 0.0)
        whole = whole - below * scaled
        result_ref[...] = jnp.where(row_ids == column, scaled, whole)
        return carry

    lax.fori_loop(0, rows, column_step, 0)


def eliminate(matrix, extra):
    source = jnp.concatenate([matrix, extra], axis=1)
    return pl.pallas_call(
        eliminate_kernel,
        out_shape=jax.ShapeDtypeStruct(source.shape, jnp.float32),
    )(source)


def factorize(rows_block, inv_cells):
    panel_rows = rows_block.shape[0] // 2
    leading = cell_sum(gram_matrix(rows_block[:panel_rows], rows_block)) * inv_cells
    eye = jnp.eye(panel_rows, dtype=jnp.float32)
    first = eliminate(leading, eye)
    first_r = first[:, :panel_rows]
    coupling = first[:, panel_rows : 2 * panel_rows]
    first_lower_inv = first[:, 2 * panel_rows :]
    first_q = mix_rows(first_lower_inv, rows_block[:panel_rows])
    remainder = rows_block[panel_rows:] - apply_rows(coupling, first_q)
    trailing = cell_sum(gram_matrix(remainder, remainder)) * inv_cells
    second = eliminate(trailing, eye)
    second_r = second[:, :panel_rows]
    second_lower_inv = second[:, panel_rows:]
    upper_rows = jnp.concatenate([first_r, coupling], axis=1)
    lower_rows = jnp.concatenate(
        [jnp.zeros((second_r.shape[0], panel_rows), jnp.float32), second_r], axis=1
    )
    triangle = jnp.concatenate([upper_rows, lower_rows], axis=0)
    return triangle, first_q, second_lower_inv, remainder


def local(orbital_block, potential):
    orb_rows = orbital_block.shape[0]
    half = orb_rows // 2
    before, after = halo_planes(orbital_block, "grid", 6)
    local_part = local_terms(orbital_block, potential)
    local_part, before, after = lax.optimization_barrier((local_part, before, after))
    first_a = filter_step(local_part, orbital_block, before, after, 1.0, start=0, count=half)
    first_b = filter_step(local_part, orbital_block, before, after, 1.0, start=half, count=orb_rows - half)
    before_a, after_a = halo_planes(first_a, "grid", 6)
    local_a = local_terms(first_a, potential)
    local_a, before_a, after_a, first_b = lax.optimization_barrier((local_a, before_a, after_a, first_b))
    before_b, after_b = halo_planes(first_b, "grid", 6)
    filtered_a = filter_step(local_a, first_a, before_a, after_a, 2.0, base=orbital_block)
    spread_a = spread_cells(filtered_a)
    local_b = local_terms(first_b, potential)
    local_b, before_b, after_b = lax.optimization_barrier((local_b, before_b, after_b))
    filtered_b = lax.optimization_barrier(
        filter_step(local_b, first_b, before_b, after_b, 2.0, base=orbital_block, base_start=half)
    )
    spread_b = spread_cells(filtered_b)
    parts, _, rows_per_part, lanes = spread_a.shape
    spread = jnp.stack([spread_a, spread_b], axis=1).reshape(-1, rows_per_part, lanes)
    inv_cells = 1.0 / (lax.axis_size("grid") * parts * rows_per_part * lanes)
    triangle, first_q, second_lower_inv, remainder = factorize(spread, inv_cells)
    second_q = mix_rows(second_lower_inv, remainder)
    orbitals = jnp.concatenate([first_q, second_q], axis=0)
    orbitals = orbitals.reshape(orbitals.shape[0], 1, rows_per_part, lanes)
    orbitals = lax.all_to_all(orbitals, "orb", 0, 1, tiled=True)
    return (orbitals.reshape(orbital_block.shape), triangle)


def solution(mesh):
    in_specs = (P("orb", "grid", None, None), P("grid", None, None))
    out_specs = (P("orb", "grid", None, None), P())
    return jax.shard_map(local, mesh=mesh, in_specs=in_specs, out_specs=out_specs, check_vma=False)
```

```python
import functools

import jax
import jax.numpy as jnp
from jax import lax
from jax.experimental import pallas as pl
from jax.experimental.pallas import tpu as pltpu
from jax.sharding import PartitionSpec as P

coefs = (
    -5369.0 / 1800.0,
    12.0 / 7.0,
    -15.0 / 56.0,
    10.0 / 189.0,
    -1.0 / 112.0,
    2.0 / 1925.0,
    -1.0 / 16632.0,
)
centre = 23.5
radius = 19.5
matmul_precision = lax.Precision.HIGH


def halo_planes(value, axis, width):
    size, length = (lax.axis_size(axis), value.shape[1])
    up = [(i, (i + 1) % size) for i in range(size - 1)]
    down = [(j, i) for i, j in up]
    last = lax.slice_in_dim(value, length - width, length, axis=1)
    first = lax.slice_in_dim(value, 0, width, axis=1)
    before = lax.ppermute(last, axis, up)
    after = lax.ppermute(first, axis, down)
    return before, after


def local_terms(orbital_field, potential):
    across = orbital_field.shape[2]
    depth_cells = orbital_field.shape[3]
    padded = jnp.pad(orbital_field, ((0, 0), (0, 0), (6, 6), (6, 6)))
    total = 3.0 * coefs[0] * orbital_field
    for k in range(1, 7):
        total = total + coefs[k] * (
            padded[:, :, 6 + k : 6 + k + across, 6 : 6 + depth_cells]
            + padded[:, :, 6 - k : 6 - k + across, 6 : 6 + depth_cells]
        )
        total = total + coefs[k] * (
            padded[:, :, 6 : 6 + across, 6 + k : 6 + k + depth_cells]
            + padded[:, :, 6 : 6 + across, 6 - k : 6 - k + depth_cells]
        )
    return -2.0 * total + potential[None] * orbital_field


def combine_kernel(scale, with_base, *refs):
    if with_base:
        local_ref, own_ref, before_ref, after_ref, base_ref, out_ref = refs
    else:
        local_ref, own_ref, before_ref, after_ref, out_ref = refs
    width = before_ref.shape[1]
    planes_own = own_ref.shape[1]

    def plane(q):
        if q < 0:
            return before_ref[:, width + q]
        if q >= planes_own:
            return after_ref[:, q - planes_own]
        return own_ref[:, q]

    for p in range(planes_own):
        acc = coefs[1] * (plane(p + 1) + plane(p - 1))
        for k in range(2, 7):
            acc = acc + coefs[k] * (plane(p + k) + plane(p - k))
        value = local_ref[:, p] - 2.0 * acc
        value = scale * (value - centre * own_ref[:, p]) / radius
        if with_base:
            value = value - base_ref[:, p]
        out_ref[:, p] = value


def filter_step(local, orbital_field, before, after, scale, base=None, start=0, count=None, base_start=0):
    count = orbital_field.shape[0] if count is None else count
    block_rows = 8 if count % 8 == 0 and start % 8 == 0 and base_start % 8 == 0 else 1
    offset = start // block_rows
    base_offset = base_start // block_rows
    block = (block_rows,) + orbital_field.shape[1:]
    halo_block = (block_rows,) + before.shape[1:]
    spec = pl.BlockSpec(block, lambda i: (i + offset, 0, 0, 0))
    halo_spec = pl.BlockSpec(halo_block, lambda i: (i + offset, 0, 0, 0))
    operands = [local, orbital_field, before, after]
    specs = [spec, spec, halo_spec, halo_spec]
    if base is not None:
        operands.append(base)
        specs.append(pl.BlockSpec(block, lambda i: (i + base_offset, 0, 0, 0)))
    return pl.pallas_call(
        functools.partial(combine_kernel, scale, base is not None),
        grid=(count // block_rows,),
        in_specs=specs,
        out_specs=pl.BlockSpec(block, lambda i: (i, 0, 0, 0)),
        out_shape=jax.ShapeDtypeStruct((count,) + orbital_field.shape[1:], jnp.float32),
    )(*operands)


def spread_cells(filtered):
    rows = filtered.shape[0]
    parts = lax.axis_size("orb")
    lanes = filtered.shape[3]
    rows_per_part = filtered.shape[1] * filtered.shape[2] // parts
    chunks = filtered.reshape(rows, parts, rows_per_part, lanes)
    return lax.all_to_all(chunks, "orb", 1, 0, tiled=True).reshape(parts, rows, rows_per_part, lanes)


def gram_matrix(left_rows, right_rows):
    return lax.dot_general(
        left_rows,
        right_rows,
        (((1, 2), (1, 2)), ((), ())),
        precision=matmul_precision,
        preferred_element_type=jnp.float32,
    )


def apply_rows(inverse, source_rows):
    return lax.dot_general(
        inverse,
        source_rows,
        (((0,), (0,)), ((), ())),
        precision=matmul_precision,
        preferred_element_type=jnp.float32,
    )


def mix_rows(weights, source_rows):
    return lax.dot_general(
        weights,
        source_rows,
        (((1,), (0,)), ((), ())),
        precision=matmul_precision,
        preferred_element_type=jnp.float32,
    )


def group_round(value, axis, stride, radix):
    size = lax.axis_size(axis)
    position = (lax.axis_index(axis) // stride) % radix
    received = [value]
    for shift in range(1, radix):
        pairs = []
        for i in range(size):
            p = (i // stride) % radix
            pairs.append((i, i + ((p + shift) % radix - p) * stride))
        received.append(lax.ppermute(value, axis, pairs))
    total = None
    for q in range(radix):
        choice = (position - q) % radix
        term = received[0]
        for shift in range(1, radix):
            term = jnp.where(choice == shift, received[shift], term)
        total = term if total is None else total + term
    return total


def exchange_sum(value, axis):
    size = lax.axis_size(axis)
    if size & (size - 1):
        return lax.psum(value, axis)
    stride = 1
    if size.bit_length() % 2 == 0:
        value = group_round(value, axis, 1, 2)
        stride = 2
    while stride < size:
        value = group_round(value, axis, stride, 4)
        stride *= 4
    return value


def cell_sum(value):
    return exchange_sum(exchange_sum(value, "grid"), "orb")


def eliminate_kernel(source_ref, result_ref):
    result_ref[...] = source_ref[...]
    rows, width = result_ref.shape
    lanes = lax.broadcasted_iota(jnp.int32, (1, width), 1)
    cols = lax.broadcasted_iota(jnp.int32, (rows, width), 1)
    row_ids = lax.broadcasted_iota(jnp.int32, (rows, 1), 0)

    def column_step(column, carry):
        current = result_ref[pl.ds(column, 1), :]
        pivot_value = jnp.sum(jnp.where(lanes == column, current, 0.0), axis=1, keepdims=True)
        inv_root = 1.0 / jnp.sqrt(pivot_value)
        scaled = jnp.where(lanes >= column, current, 0.0) * inv_root
        whole = result_ref[...]
        below = jnp.sum(jnp.where(cols == column, whole, 0.0), axis=1, keepdims=True) * inv_root
        below = jnp.where(row_ids > column, below, 0.0)
        whole = whole - below * scaled
        result_ref[...] = jnp.where(row_ids == column, scaled, whole)
        return carry

    lax.fori_loop(0, rows, column_step, 0)


def eliminate(matrix, extra):
    source = jnp.concatenate([matrix, extra], axis=1)
    return pl.pallas_call(
        eliminate_kernel,
        out_shape=jax.ShapeDtypeStruct(source.shape, jnp.float32),
    )(source)


def factorize(rows_block, inv_cells):
    panel_rows = rows_block.shape[0] // 2
    leading = cell_sum(gram_matrix(rows_block[:panel_rows], rows_block)) * inv_cells
    eye = jnp.eye(panel_rows, dtype=jnp.float32)
    first = eliminate(leading, eye)
    first_r = first[:, :panel_rows]
    coupling = first[:, panel_rows : 2 * panel_rows]
    first_lower_inv = first[:, 2 * panel_rows :]
    first_q = mix_rows(first_lower_inv, rows_block[:panel_rows])
    remainder = rows_block[panel_rows:] - apply_rows(coupling, first_q)
    trailing = cell_sum(gram_matrix(remainder, remainder)) * inv_cells
    second = eliminate(trailing, eye)
    second_r = second[:, :panel_rows]
    second_lower_inv = second[:, panel_rows:]
    upper_rows = jnp.concatenate([first_r, coupling], axis=1)
    lower_rows = jnp.concatenate(
        [jnp.zeros((second_r.shape[0], panel_rows), jnp.float32), second_r], axis=1
    )
    triangle = jnp.concatenate([upper_rows, lower_rows], axis=0)
    return triangle, first_q, second_lower_inv, remainder


def local(orbital_block, potential):
    orb_rows = orbital_block.shape[0]
    half = orb_rows // 2
    before, after = halo_planes(orbital_block, "grid", 6)
    local_part = local_terms(orbital_block, potential)
    local_part, before, after = lax.optimization_barrier((local_part, before, after))
    first_a = filter_step(local_part, orbital_block, before, after, 1.0, start=0, count=half)
    first_b = filter_step(local_part, orbital_block, before, after, 1.0, start=half, count=orb_rows - half)
    before_a, after_a = halo_planes(first_a, "grid", 6)
    local_a = local_terms(first_a, potential)
    local_a, before_a, after_a, first_b = lax.optimization_barrier((local_a, before_a, after_a, first_b))
    before_b, after_b = halo_planes(first_b, "grid", 6)
    filtered_a = filter_step(local_a, first_a, before_a, after_a, 2.0, base=orbital_block)
    spread_a = spread_cells(filtered_a)
    local_b = local_terms(first_b, potential)
    local_b, before_b, after_b = lax.optimization_barrier((local_b, before_b, after_b))
    filtered_b = lax.optimization_barrier(
        filter_step(local_b, first_b, before_b, after_b, 2.0, base=orbital_block, base_start=half)
    )
    spread_b = spread_cells(filtered_b)
    parts, _, rows_per_part, lanes = spread_a.shape
    spread = jnp.stack([spread_a, spread_b], axis=1).reshape(-1, rows_per_part, lanes)
    inv_cells = 1.0 / (lax.axis_size("grid") * parts * rows_per_part * lanes)
    triangle, first_q, second_lower_inv, remainder = factorize(spread, inv_cells)
    second_q = mix_rows(second_lower_inv, remainder)
    orbitals = jnp.concatenate([first_q, second_q], axis=0)
    orbitals = orbitals.reshape(orbitals.shape[0], 1, rows_per_part, lanes)
    orbitals = lax.all_to_all(orbitals, "orb", 0, 1, tiled=True)
    return (orbitals.reshape(orbital_block.shape), triangle)


def solution(mesh):
    in_specs = (P("orb", "grid", None, None), P("grid", None, None))
    out_specs = (P("orb", "grid", None, None), P())
    return jax.shard_map(local, mesh=mesh, in_specs=in_specs, out_specs=out_specs, check_vma=False)
```

```python
import functools

import jax
import jax.numpy as jnp
from jax import lax
from jax.experimental import pallas as pl
from jax.experimental.pallas import tpu as pltpu
from jax.sharding import PartitionSpec as P

coefs = (
    -5369.0 / 1800.0,
    12.0 / 7.0,
    -15.0 / 56.0,
    10.0 / 189.0,
    -1.0 / 112.0,
    2.0 / 1925.0,
    -1.0 / 16632.0,
)
centre = 23.5
radius = 19.5
matmul_precision = lax.Precision.HIGH


def halo_planes(value, axis, width):
    size, length = (lax.axis_size(axis), value.shape[1])
    up = [(i, (i + 1) % size) for i in range(size - 1)]
    down = [(j, i) for i, j in up]
    last = lax.slice_in_dim(value, length - width, length, axis=1)
    first = lax.slice_in_dim(value, 0, width, axis=1)
    before = lax.ppermute(last, axis, up)
    after = lax.ppermute(first, axis, down)
    return before, after


def local_terms(orbital_field, potential):
    across = orbital_field.shape[2]
    depth_cells = orbital_field.shape[3]
    padded = jnp.pad(orbital_field, ((0, 0), (0, 0), (6, 6), (6, 6)))
    total = 3.0 * coefs[0] * orbital_field
    for k in range(1, 7):
        total = total + coefs[k] * (
            padded[:, :, 6 + k : 6 + k + across, 6 : 6 + depth_cells]
            + padded[:, :, 6 - k : 6 - k + across, 6 : 6 + depth_cells]
        )
        total = total + coefs[k] * (
            padded[:, :, 6 : 6 + across, 6 + k : 6 + k + depth_cells]
            + padded[:, :, 6 : 6 + across, 6 - k : 6 - k + depth_cells]
        )
    return -2.0 * total + potential[None] * orbital_field


def combine_kernel(scale, with_base, *refs):
    if with_base:
        local_ref, own_ref, before_ref, after_ref, base_ref, out_ref = refs
    else:
        local_ref, own_ref, before_ref, after_ref, out_ref = refs
    width = before_ref.shape[1]
    planes_own = own_ref.shape[1]

    def plane(q):
        if q < 0:
            return before_ref[:, width + q]
        if q >= planes_own:
            return after_ref[:, q - planes_own]
        return own_ref[:, q]

    for p in range(planes_own):
        acc = coefs[1] * (plane(p + 1) + plane(p - 1))
        for k in range(2, 7):
            acc = acc + coefs[k] * (plane(p + k) + plane(p - k))
        value = local_ref[:, p] - 2.0 * acc
        value = scale * (value - centre * own_ref[:, p]) / radius
        if with_base:
            value = value - base_ref[:, p]
        out_ref[:, p] = value


def filter_step(local, orbital_field, before, after, scale, base=None, start=0, count=None, base_start=0):
    count = orbital_field.shape[0] if count is None else count
    block_rows = 8 if count % 8 == 0 and start % 8 == 0 and base_start % 8 == 0 else 1
    offset = start // block_rows
    base_offset = base_start // block_rows
    block = (block_rows,) + orbital_field.shape[1:]
    halo_block = (block_rows,) + before.shape[1:]
    spec = pl.BlockSpec(block, lambda i: (i + offset, 0, 0, 0))
    halo_spec = pl.BlockSpec(halo_block, lambda i: (i + offset, 0, 0, 0))
    operands = [local, orbital_field, before, after]
    specs = [spec, spec, halo_spec, halo_spec]
    if base is not None:
        operands.append(base)
        specs.append(pl.BlockSpec(block, lambda i: (i + base_offset, 0, 0, 0)))
    return pl.pallas_call(
        functools.partial(combine_kernel, scale, base is not None),
        grid=(count // block_rows,),
        in_specs=specs,
        out_specs=pl.BlockSpec(block, lambda i: (i, 0, 0, 0)),
        out_shape=jax.ShapeDtypeStruct((count,) + orbital_field.shape[1:], jnp.float32),
    )(*operands)


def spread_cells(filtered):
    rows = filtered.shape[0]
    parts = lax.axis_size("orb")
    lanes = filtered.shape[3]
    rows_per_part = filtered.shape[1] * filtered.shape[2] // parts
    chunks = filtered.reshape(rows, parts, rows_per_part, lanes)
    return lax.all_to_all(chunks, "orb", 1, 0, tiled=True).reshape(parts, rows, rows_per_part, lanes)


def gram_matrix(left_rows, right_rows):
    return lax.dot_general(
        left_rows,
        right_rows,
        (((1, 2), (1, 2)), ((), ())),
        precision=matmul_precision,
        preferred_element_type=jnp.float32,
    )


def apply_rows(inverse, source_rows):
    return lax.dot_general(
        inverse,
        source_rows,
        (((0,), (0,)), ((), ())),
        precision=matmul_precision,
        preferred_element_type=jnp.float32,
    )


def mix_rows(weights, source_rows):
    return lax.dot_general(
        weights,
        source_rows,
        (((1,), (0,)), ((), ())),
        precision=matmul_precision,
        preferred_element_type=jnp.float32,
    )


def group_round(value, axis, stride, radix):
    size = lax.axis_size(axis)
    position = (lax.axis_index(axis) // stride) % radix
    received = [value]
    for shift in range(1, radix):
        pairs = []
        for i in range(size):
            p = (i // stride) % radix
            pairs.append((i, i + ((p + shift) % radix - p) * stride))
        received.append(lax.ppermute(value, axis, pairs))
    total = None
    for q in range(radix):
        choice = (position - q) % radix
        term = received[0]
        for shift in range(1, radix):
            term = jnp.where(choice == shift, received[shift], term)
        total = term if total is None else total + term
    return total


def exchange_sum(value, axis):
    size = lax.axis_size(axis)
    if size & (size - 1):
        return lax.psum(value, axis)
    stride = 1
    if size.bit_length() % 2 == 0:
        value = group_round(value, axis, 1, 2)
        stride = 2
    while stride < size:
        value = group_round(value, axis, stride, 4)
        stride *= 4
    return value


def cell_sum(value):
    return exchange_sum(exchange_sum(value, "grid"), "orb")


def eliminate_kernel(source_ref, result_ref):
    result_ref[...] = source_ref[...]
    rows, width = result_ref.shape
    lanes = lax.broadcasted_iota(jnp.int32, (1, width), 1)
    cols = lax.broadcasted_iota(jnp.int32, (rows, width), 1)
    row_ids = lax.broadcasted_iota(jnp.int32, (rows, 1), 0)

    def column_step(column, carry):
        current = result_ref[pl.ds(column, 1), :]
        pivot_value = jnp.sum(jnp.where(lanes == column, current, 0.0), axis=1, keepdims=True)
        inv_root = 1.0 / jnp.sqrt(pivot_value)
        scaled = jnp.where(lanes >= column, current, 0.0) * inv_root
        whole = result_ref[...]
        below = jnp.sum(jnp.where(cols == column, whole, 0.0), axis=1, keepdims=True) * inv_root
        below = jnp.where(row_ids > column, below, 0.0)
        whole = whole - below * scaled
        result_ref[...] = jnp.where(row_ids == column, scaled, whole)
        return carry

    lax.fori_loop(0, rows, column_step, 0)


def eliminate(matrix, extra):
    source = jnp.concatenate([matrix, extra], axis=1)
    return pl.pallas_call(
        eliminate_kernel,
        out_shape=jax.ShapeDtypeStruct(source.shape, jnp.float32),
    )(source)


def factorize(rows_block, inv_cells):
    panel_rows = rows_block.shape[0] // 2
    leading = cell_sum(gram_matrix(rows_block[:panel_rows], rows_block)) * inv_cells
    eye = jnp.eye(panel_rows, dtype=jnp.float32)
    first = eliminate(leading, eye)
    first_r = first[:, :panel_rows]
    coupling = first[:, panel_rows : 2 * panel_rows]
    first_lower_inv = first[:, 2 * panel_rows :]
    first_q = mix_rows(first_lower_inv, rows_block[:panel_rows])
    zeros = jnp.zeros((panel_rows, panel_rows), jnp.float32)
    lift = jnp.concatenate([zeros, coupling.T], axis=0)
    adjusted = rows_block - mix_rows(lift, first_q)
    remainder = adjusted[panel_rows:]
    trailing = cell_sum(gram_matrix(remainder, remainder)) * inv_cells
    second = eliminate(trailing, eye)
    second_r = second[:, :panel_rows]
    second_lower_inv = second[:, panel_rows:]
    upper_rows = jnp.concatenate([first_r, coupling], axis=1)
    lower_rows = jnp.concatenate([zeros, second_r], axis=1)
    triangle = jnp.concatenate([upper_rows, lower_rows], axis=0)
    weights = jnp.concatenate(
        [
            jnp.concatenate([first_lower_inv, zeros], axis=1),
            jnp.concatenate([zeros, second_lower_inv], axis=1),
        ],
        axis=0,
    )
    return triangle, mix_rows(weights, adjusted)


def local(orbital_block, potential):
    orb_rows = orbital_block.shape[0]
    half = orb_rows // 2
    before, after = halo_planes(orbital_block, "grid", 6)
    local_part = local_terms(orbital_block, potential)
    local_part, before, after = lax.optimization_barrier((local_part, before, after))
    first_a = filter_step(local_part, orbital_block, before, after, 1.0, start=0, count=half)
    first_b = filter_step(local_part, orbital_block, before, after, 1.0, start=half, count=orb_rows - half)
    before_a, after_a = halo_planes(first_a, "grid", 6)
    local_a = local_terms(first_a, potential)
    local_a, before_a, after_a, first_b = lax.optimization_barrier((local_a, before_a, after_a, first_b))
    before_b, after_b = halo_planes(first_b, "grid", 6)
    filtered_a = filter_step(local_a, first_a, before_a, after_a, 2.0, base=orbital_block)
    spread_a = spread_cells(filtered_a)
    local_b = local_terms(first_b, potential)
    local_b, before_b, after_b = lax.optimization_barrier((local_b, before_b, after_b))
    filtered_b = lax.optimization_barrier(
        filter_step(local_b, first_b, before_b, after_b, 2.0, base=orbital_block, base_start=half)
    )
    spread_b = spread_cells(filtered_b)
    parts, _, rows_per_part, lanes = spread_a.shape
    spread = jnp.stack([spread_a, spread_b], axis=1).reshape(-1, rows_per_part, lanes)
    inv_cells = 1.0 / (lax.axis_size("grid") * parts * rows_per_part * lanes)
    triangle, orbitals = factorize(spread, inv_cells)
    orbitals = orbitals.reshape(orbitals.shape[0], 1, rows_per_part, lanes)
    orbitals = lax.all_to_all(orbitals, "orb", 0, 1, tiled=True)
    return (orbitals.reshape(orbital_block.shape), triangle)


def solution(mesh):
    in_specs = (P("orb", "grid", None, None), P("grid", None, None))
    out_specs = (P("orb", "grid", None, None), P())
    return jax.shard_map(local, mesh=mesh, in_specs=in_specs, out_specs=out_specs, check_vma=False)
```

```python
import functools

import jax
import jax.numpy as jnp
from jax import lax
from jax.experimental import pallas as pl
from jax.experimental.pallas import tpu as pltpu
from jax.sharding import PartitionSpec as P

coefs = (
    -5369.0 / 1800.0,
    12.0 / 7.0,
    -15.0 / 56.0,
    10.0 / 189.0,
    -1.0 / 112.0,
    2.0 / 1925.0,
    -1.0 / 16632.0,
)
centre = 23.5
radius = 19.5
matmul_precision = lax.Precision.HIGH


def halo_planes(value, axis, width):
    size, length = (lax.axis_size(axis), value.shape[1])
    up = [(i, (i + 1) % size) for i in range(size - 1)]
    down = [(j, i) for i, j in up]
    last = lax.slice_in_dim(value, length - width, length, axis=1)
    first = lax.slice_in_dim(value, 0, width, axis=1)
    before = lax.ppermute(last, axis, up)
    after = lax.ppermute(first, axis, down)
    return before, after


def local_terms(orbital_field, potential):
    across = orbital_field.shape[2]
    depth_cells = orbital_field.shape[3]
    padded = jnp.pad(orbital_field, ((0, 0), (0, 0), (6, 6), (6, 6)))
    total = 3.0 * coefs[0] * orbital_field
    for k in range(1, 7):
        total = total + coefs[k] * (
            padded[:, :, 6 + k : 6 + k + across, 6 : 6 + depth_cells]
            + padded[:, :, 6 - k : 6 - k + across, 6 : 6 + depth_cells]
        )
        total = total + coefs[k] * (
            padded[:, :, 6 : 6 + across, 6 + k : 6 + k + depth_cells]
            + padded[:, :, 6 : 6 + across, 6 - k : 6 - k + depth_cells]
        )
    return -2.0 * total + potential[None] * orbital_field


def combine_kernel(scale, with_base, *refs):
    if with_base:
        local_ref, own_ref, before_ref, after_ref, base_ref, out_ref = refs
    else:
        local_ref, own_ref, before_ref, after_ref, out_ref = refs
    width = before_ref.shape[1]
    planes_own = own_ref.shape[1]

    def plane(q):
        if q < 0:
            return before_ref[:, width + q]
        if q >= planes_own:
            return after_ref[:, q - planes_own]
        return own_ref[:, q]

    for p in range(planes_own):
        acc = coefs[1] * (plane(p + 1) + plane(p - 1))
        for k in range(2, 7):
            acc = acc + coefs[k] * (plane(p + k) + plane(p - k))
        value = local_ref[:, p] - 2.0 * acc
        value = scale * (value - centre * own_ref[:, p]) / radius
        if with_base:
            value = value - base_ref[:, p]
        out_ref[:, p] = value


def filter_step(
    local, orbital_field, before, after, scale, base=None, start=0, count=None, base_start=0, halo_start=None
):
    count = orbital_field.shape[0] if count is None else count
    halo_start = start if halo_start is None else halo_start
    aligned = all(value % 8 == 0 for value in (count, start, base_start, halo_start))
    block_rows = 8 if aligned else 1
    offset = start // block_rows
    halo_offset = halo_start // block_rows
    base_offset = base_start // block_rows
    block = (block_rows,) + orbital_field.shape[1:]
    halo_block = (block_rows,) + before.shape[1:]
    spec = pl.BlockSpec(block, lambda i: (i + offset, 0, 0, 0))
    halo_spec = pl.BlockSpec(halo_block, lambda i: (i + halo_offset, 0, 0, 0))
    operands = [local, orbital_field, before, after]
    specs = [spec, spec, halo_spec, halo_spec]
    if base is not None:
        operands.append(base)
        specs.append(pl.BlockSpec(block, lambda i: (i + base_offset, 0, 0, 0)))
    return pl.pallas_call(
        functools.partial(combine_kernel, scale, base is not None),
        grid=(count // block_rows,),
        in_specs=specs,
        out_specs=pl.BlockSpec(block, lambda i: (i, 0, 0, 0)),
        out_shape=jax.ShapeDtypeStruct((count,) + orbital_field.shape[1:], jnp.float32),
    )(*operands)


def spread_cells(filtered):
    rows = filtered.shape[0]
    parts = lax.axis_size("orb")
    lanes = filtered.shape[3]
    rows_per_part = filtered.shape[1] * filtered.shape[2] // parts
    chunks = filtered.reshape(rows, parts, rows_per_part, lanes)
    return lax.all_to_all(chunks, "orb", 1, 0, tiled=True).reshape(parts, rows, rows_per_part, lanes)


def gram_matrix(left_rows, right_rows):
    return lax.dot_general(
        left_rows,
        right_rows,
        (((1, 2), (1, 2)), ((), ())),
        precision=matmul_precision,
        preferred_element_type=jnp.float32,
    )


def apply_rows(inverse, source_rows):
    return lax.dot_general(
        inverse,
        source_rows,
        (((0,), (0,)), ((), ())),
        precision=matmul_precision,
        preferred_element_type=jnp.float32,
    )


def mix_rows(weights, source_rows):
    return lax.dot_general(
        weights,
        source_rows,
        (((1,), (0,)), ((), ())),
        precision=matmul_precision,
        preferred_element_type=jnp.float32,
    )


def group_round(value, axis, stride, radix):
    size = lax.axis_size(axis)
    position = (lax.axis_index(axis) // stride) % radix
    received = [value]
    for shift in range(1, radix):
        pairs = []
        for i in range(size):
            p = (i // stride) % radix
            pairs.append((i, i + ((p + shift) % radix - p) * stride))
        received.append(lax.ppermute(value, axis, pairs))
    total = None
    for q in range(radix):
        choice = (position - q) % radix
        term = received[0]
        for shift in range(1, radix):
            term = jnp.where(choice == shift, received[shift], term)
        total = term if total is None else total + term
    return total


def exchange_sum(value, axis):
    size = lax.axis_size(axis)
    if size & (size - 1):
        return lax.psum(value, axis)
    stride = 1
    if size.bit_length() % 2 == 0:
        value = group_round(value, axis, 1, 2)
        stride = 2
    while stride < size:
        value = group_round(value, axis, stride, 4)
        stride *= 4
    return value


def cell_sum(value):
    return exchange_sum(exchange_sum(value, "grid"), "orb")


def eliminate_kernel(source_ref, result_ref):
    result_ref[...] = source_ref[...]
    rows, width = result_ref.shape
    lanes = lax.broadcasted_iota(jnp.int32, (1, width), 1)
    cols = lax.broadcasted_iota(jnp.int32, (rows, width), 1)
    row_ids = lax.broadcasted_iota(jnp.int32, (rows, 1), 0)

    def column_step(column, carry):
        current = result_ref[pl.ds(column, 1), :]
        pivot_value = jnp.sum(jnp.where(lanes == column, current, 0.0), axis=1, keepdims=True)
        inv_root = 1.0 / jnp.sqrt(pivot_value)
        scaled = jnp.where(lanes >= column, current, 0.0) * inv_root
        whole = result_ref[...]
        below = jnp.sum(jnp.where(cols == column, whole, 0.0), axis=1, keepdims=True) * inv_root
        below = jnp.where(row_ids > column, below, 0.0)
        whole = whole - below * scaled
        result_ref[...] = jnp.where(row_ids == column, scaled, whole)
        return carry

    lax.fori_loop(0, rows, column_step, 0)


def eliminate(matrix, extra):
    source = jnp.concatenate([matrix, extra], axis=1)
    return pl.pallas_call(
        eliminate_kernel,
        out_shape=jax.ShapeDtypeStruct(source.shape, jnp.float32),
    )(source)


def factorize(rows_block, inv_cells):
    panel_rows = rows_block.shape[0] // 2
    leading = cell_sum(gram_matrix(rows_block[:panel_rows], rows_block)) * inv_cells
    eye = jnp.eye(panel_rows, dtype=jnp.float32)
    first = eliminate(leading, eye)
    first_r = first[:, :panel_rows]
    coupling = first[:, panel_rows : 2 * panel_rows]
    first_lower_inv = first[:, 2 * panel_rows :]
    first_q = mix_rows(first_lower_inv, rows_block[:panel_rows])
    remainder = rows_block[panel_rows:] - apply_rows(coupling, first_q)
    trailing = cell_sum(gram_matrix(remainder, remainder)) * inv_cells
    second = eliminate(trailing, eye)
    second_r = second[:, :panel_rows]
    second_lower_inv = second[:, panel_rows:]
    upper_rows = jnp.concatenate([first_r, coupling], axis=1)
    lower_rows = jnp.concatenate(
        [jnp.zeros((second_r.shape[0], panel_rows), jnp.float32), second_r], axis=1
    )
    triangle = jnp.concatenate([upper_rows, lower_rows], axis=0)
    return triangle, first_q, second_lower_inv, remainder


def local(orbital_block, potential):
    orb_rows = orbital_block.shape[0]
    half = orb_rows // 2
    local_part = local_terms(orbital_block, potential)
    before_0, after_0 = halo_planes(orbital_block[:half], "grid", 6)
    local_part, before_0, after_0 = lax.optimization_barrier((local_part, before_0, after_0))
    second_rows, before_0, after_0 = lax.optimization_barrier((orbital_block[half:], before_0, after_0))
    before_1, after_1 = halo_planes(second_rows, "grid", 6)
    first_a = filter_step(local_part, orbital_block, before_0, after_0, 1.0, start=0, count=half)
    before_1, after_1 = lax.optimization_barrier((before_1, after_1))
    first_b = filter_step(
        local_part, orbital_block, before_1, after_1, 1.0, start=half, count=orb_rows - half, halo_start=0
    )
    before_a, after_a = halo_planes(first_a, "grid", 6)
    local_a = local_terms(first_a, potential)
    local_a, before_a, after_a, first_b = lax.optimization_barrier((local_a, before_a, after_a, first_b))
    before_b, after_b = halo_planes(first_b, "grid", 6)
    filtered_a = filter_step(local_a, first_a, before_a, after_a, 2.0, base=orbital_block)
    spread_a = spread_cells(filtered_a)
    local_b = local_terms(first_b, potential)
    local_b, before_b, after_b = lax.optimization_barrier((local_b, before_b, after_b))
    filtered_b = lax.optimization_barrier(
        filter_step(local_b, first_b, before_b, after_b, 2.0, base=orbital_block, base_start=half)
    )
    spread_b = spread_cells(filtered_b)
    parts, _, rows_per_part, lanes = spread_a.shape
    spread = jnp.stack([spread_a, spread_b], axis=1).reshape(-1, rows_per_part, lanes)
    inv_cells = 1.0 / (lax.axis_size("grid") * parts * rows_per_part * lanes)
    triangle, first_q, second_lower_inv, remainder = factorize(spread, inv_cells)
    second_q = mix_rows(second_lower_inv, remainder)
    orbitals = jnp.concatenate([first_q, second_q], axis=0)
    orbitals = orbitals.reshape(orbitals.shape[0], 1, rows_per_part, lanes)
    orbitals = lax.all_to_all(orbitals, "orb", 0, 1, tiled=True)
    return (orbitals.reshape(orbital_block.shape), triangle)


def solution(mesh):
    in_specs = (P("orb", "grid", None, None), P("grid", None, None))
    out_specs = (P("orb", "grid", None, None), P())
    return jax.shard_map(local, mesh=mesh, in_specs=in_specs, out_specs=out_specs, check_vma=False)
```

```python
import functools

import jax
import jax.numpy as jnp
from jax import lax
from jax.experimental import pallas as pl
from jax.experimental.pallas import tpu as pltpu
from jax.sharding import PartitionSpec as P

coefs = (
    -5369.0 / 1800.0,
    12.0 / 7.0,
    -15.0 / 56.0,
    10.0 / 189.0,
    -1.0 / 112.0,
    2.0 / 1925.0,
    -1.0 / 16632.0,
)
centre = 23.5
radius = 19.5
matmul_precision = lax.Precision.HIGH


def halo_planes(value, axis, width):
    size, length = (lax.axis_size(axis), value.shape[1])
    up = [(i, (i + 1) % size) for i in range(size - 1)]
    down = [(j, i) for i, j in up]
    last = lax.slice_in_dim(value, length - width, length, axis=1)
    first = lax.slice_in_dim(value, 0, width, axis=1)
    before = lax.ppermute(last, axis, up)
    after = lax.ppermute(first, axis, down)
    return before, after


def local_terms(orbital_field, potential):
    across = orbital_field.shape[2]
    depth_cells = orbital_field.shape[3]
    padded = jnp.pad(orbital_field, ((0, 0), (0, 0), (6, 6), (6, 6)))
    total = 3.0 * coefs[0] * orbital_field
    for k in range(1, 7):
        total = total + coefs[k] * (
            padded[:, :, 6 + k : 6 + k + across, 6 : 6 + depth_cells]
            + padded[:, :, 6 - k : 6 - k + across, 6 : 6 + depth_cells]
        )
        total = total + coefs[k] * (
            padded[:, :, 6 : 6 + across, 6 + k : 6 + k + depth_cells]
            + padded[:, :, 6 : 6 + across, 6 - k : 6 - k + depth_cells]
        )
    return -2.0 * total + potential[None] * orbital_field


def combine_kernel(scale, with_base, *refs):
    if with_base:
        local_ref, own_ref, before_ref, after_ref, base_ref, out_ref = refs
    else:
        local_ref, own_ref, before_ref, after_ref, out_ref = refs
    width = before_ref.shape[1]
    planes_own = own_ref.shape[1]

    def plane(q):
        if q < 0:
            return before_ref[:, width + q]
        if q >= planes_own:
            return after_ref[:, q - planes_own]
        return own_ref[:, q]

    for p in range(planes_own):
        acc = coefs[1] * (plane(p + 1) + plane(p - 1))
        for k in range(2, 7):
            acc = acc + coefs[k] * (plane(p + k) + plane(p - k))
        value = local_ref[:, p] - 2.0 * acc
        value = scale * (value - centre * own_ref[:, p]) / radius
        if with_base:
            value = value - base_ref[:, p]
        out_ref[:, p] = value


def filter_step(
    local, orbital_field, before, after, scale, base=None, start=0, count=None, base_start=0, halo_start=None
):
    count = orbital_field.shape[0] if count is None else count
    halo_start = start if halo_start is None else halo_start
    aligned = all(value % 8 == 0 for value in (count, start, base_start, halo_start))
    block_rows = 8 if aligned else 1
    offset = start // block_rows
    halo_offset = halo_start // block_rows
    base_offset = base_start // block_rows
    block = (block_rows,) + orbital_field.shape[1:]
    halo_block = (block_rows,) + before.shape[1:]
    spec = pl.BlockSpec(block, lambda i: (i + offset, 0, 0, 0))
    halo_spec = pl.BlockSpec(halo_block, lambda i: (i + halo_offset, 0, 0, 0))
    operands = [local, orbital_field, before, after]
    specs = [spec, spec, halo_spec, halo_spec]
    if base is not None:
        operands.append(base)
        specs.append(pl.BlockSpec(block, lambda i: (i + base_offset, 0, 0, 0)))
    return pl.pallas_call(
        functools.partial(combine_kernel, scale, base is not None),
        grid=(count // block_rows,),
        in_specs=specs,
        out_specs=pl.BlockSpec(block, lambda i: (i, 0, 0, 0)),
        out_shape=jax.ShapeDtypeStruct((count,) + orbital_field.shape[1:], jnp.float32),
    )(*operands)


def spread_cells(filtered):
    rows = filtered.shape[0]
    parts = lax.axis_size("orb")
    lanes = filtered.shape[3]
    rows_per_part = filtered.shape[1] * filtered.shape[2] // parts
    chunks = filtered.reshape(rows, parts, rows_per_part, lanes)
    return lax.all_to_all(chunks, "orb", 1, 0, tiled=True).reshape(parts, rows, rows_per_part, lanes)


def gram_matrix(left_rows, right_rows):
    return lax.dot_general(
        left_rows,
        right_rows,
        (((1, 2), (1, 2)), ((), ())),
        precision=matmul_precision,
        preferred_element_type=jnp.float32,
    )


def apply_rows(inverse, source_rows):
    return lax.dot_general(
        inverse,
        source_rows,
        (((0,), (0,)), ((), ())),
        precision=matmul_precision,
        preferred_element_type=jnp.float32,
    )


def mix_rows(weights, source_rows):
    return lax.dot_general(
        weights,
        source_rows,
        (((1,), (0,)), ((), ())),
        precision=matmul_precision,
        preferred_element_type=jnp.float32,
    )


def group_round(value, axis, stride, radix):
    size = lax.axis_size(axis)
    position = (lax.axis_index(axis) // stride) % radix
    received = [value]
    for shift in range(1, radix):
        pairs = []
        for i in range(size):
            p = (i // stride) % radix
            pairs.append((i, i + ((p + shift) % radix - p) * stride))
        received.append(lax.ppermute(value, axis, pairs))
    total = None
    for q in range(radix):
        choice = (position - q) % radix
        term = received[0]
        for shift in range(1, radix):
            term = jnp.where(choice == shift, received[shift], term)
        total = term if total is None else total + term
    return total


def exchange_sum(value, axis):
    size = lax.axis_size(axis)
    if size & (size - 1):
        return lax.psum(value, axis)
    stride = 1
    if size.bit_length() % 2 == 0:
        value = group_round(value, axis, 1, 2)
        stride = 2
    while stride < size:
        value = group_round(value, axis, stride, 4)
        stride *= 4
    return value


def cell_sum(value):
    return exchange_sum(exchange_sum(value, "grid"), "orb")


def eliminate_kernel(source_ref, result_ref):
    result_ref[...] = source_ref[...]
    rows, width = result_ref.shape
    lanes = lax.broadcasted_iota(jnp.int32, (1, width), 1)
    cols = lax.broadcasted_iota(jnp.int32, (rows, width), 1)
    row_ids = lax.broadcasted_iota(jnp.int32, (rows, 1), 0)

    def column_step(column, carry):
        current = result_ref[pl.ds(column, 1), :]
        pivot_value = jnp.sum(jnp.where(lanes == column, current, 0.0), axis=1, keepdims=True)
        inv_root = 1.0 / jnp.sqrt(pivot_value)
        scaled = jnp.where(lanes >= column, current, 0.0) * inv_root
        whole = result_ref[...]
        below = jnp.sum(jnp.where(cols == column, whole, 0.0), axis=1, keepdims=True) * inv_root
        below = jnp.where(row_ids > column, below, 0.0)
        whole = whole - below * scaled
        result_ref[...] = jnp.where(row_ids == column, scaled, whole)
        return carry

    lax.fori_loop(0, rows, column_step, 0)


def eliminate(matrix, extra):
    source = jnp.concatenate([matrix, extra], axis=1)
    return pl.pallas_call(
        eliminate_kernel,
        out_shape=jax.ShapeDtypeStruct(source.shape, jnp.float32),
    )(source)


def factorize(rows_block, inv_cells):
    panel_rows = rows_block.shape[0] // 2
    leading = cell_sum(gram_matrix(rows_block[:panel_rows], rows_block)) * inv_cells
    eye = jnp.eye(panel_rows, dtype=jnp.float32)
    first = eliminate(leading, eye)
    first_r = first[:, :panel_rows]
    coupling = first[:, panel_rows : 2 * panel_rows]
    first_lower_inv = first[:, 2 * panel_rows :]
    first_q = mix_rows(first_lower_inv, rows_block[:panel_rows])
    remainder = rows_block[panel_rows:] - apply_rows(coupling, first_q)
    trailing = cell_sum(gram_matrix(remainder, remainder)) * inv_cells
    second = eliminate(trailing, eye)
    second_r = second[:, :panel_rows]
    second_lower_inv = second[:, panel_rows:]
    upper_rows = jnp.concatenate([first_r, coupling], axis=1)
    lower_rows = jnp.concatenate(
        [jnp.zeros((second_r.shape[0], panel_rows), jnp.float32), second_r], axis=1
    )
    triangle = jnp.concatenate([upper_rows, lower_rows], axis=0)
    return triangle, first_q, second_lower_inv, remainder


def local(orbital_block, potential):
    orb_rows = orbital_block.shape[0]
    half = orb_rows // 2
    local_part = local_terms(orbital_block, potential)
    before_0, after_0 = halo_planes(orbital_block[:half], "grid", 6)
    local_part, before_0, after_0 = lax.optimization_barrier((local_part, before_0, after_0))
    second_rows, before_0, after_0 = lax.optimization_barrier((orbital_block[half:], before_0, after_0))
    before_1, after_1 = halo_planes(second_rows, "grid", 6)
    piece = half // 2 if half % 16 == 0 else half
    firsts = []
    for start in range(0, orb_rows, piece):
        before, after = (before_0, after_0) if start < half else (before_1, after_1)
        halo_start = start if start < half else start - half
        if start == half:
            before_1, after_1 = lax.optimization_barrier((before_1, after_1))
            before, after = before_1, after_1
        firsts.append(
            filter_step(
                local_part, orbital_block, before, after, 1.0, start=start, count=piece, halo_start=halo_start
            )
        )
    spreads = []
    received = None
    for index, first in enumerate(firsts):
        if received is not None:
            first, *received = lax.optimization_barrier((first,) + received)
        before, after = halo_planes(first, "grid", 6)
        local_piece = local_terms(first, potential)
        local_piece, before, after = lax.optimization_barrier((local_piece, before, after))
        received = (before, after)
        filtered = filter_step(
            local_piece, first, before, after, 2.0, base=orbital_block, base_start=index * piece
        )
        spreads.append(spread_cells(lax.optimization_barrier(filtered)))
    spread_a = spreads[0]
    parts, _, rows_per_part, lanes = spread_a.shape
    spread = jnp.stack(spreads, axis=1).reshape(-1, rows_per_part, lanes)
    inv_cells = 1.0 / (lax.axis_size("grid") * parts * rows_per_part * lanes)
    triangle, first_q, second_lower_inv, remainder = factorize(spread, inv_cells)
    second_q = mix_rows(second_lower_inv, remainder)
    orbitals = jnp.concatenate([first_q, second_q], axis=0)
    orbitals = orbitals.reshape(orbitals.shape[0], 1, rows_per_part, lanes)
    orbitals = lax.all_to_all(orbitals, "orb", 0, 1, tiled=True)
    return (orbitals.reshape(orbital_block.shape), triangle)


def solution(mesh):
    in_specs = (P("orb", "grid", None, None), P("grid", None, None))
    out_specs = (P("orb", "grid", None, None), P())
    return jax.shard_map(local, mesh=mesh, in_specs=in_specs, out_specs=out_specs, check_vma=False)
```

```python
import functools

import jax
import jax.numpy as jnp
from jax import lax
from jax.experimental import pallas as pl
from jax.experimental.pallas import tpu as pltpu
from jax.sharding import PartitionSpec as P

coefs = (
    -5369.0 / 1800.0,
    12.0 / 7.0,
    -15.0 / 56.0,
    10.0 / 189.0,
    -1.0 / 112.0,
    2.0 / 1925.0,
    -1.0 / 16632.0,
)
centre = 23.5
radius = 19.5
matmul_precision = lax.Precision.HIGH


def halo_planes(value, axis, width):
    size, length = (lax.axis_size(axis), value.shape[1])
    up = [(i, (i + 1) % size) for i in range(size - 1)]
    down = [(j, i) for i, j in up]
    last = lax.slice_in_dim(value, length - width, length, axis=1)
    first = lax.slice_in_dim(value, 0, width, axis=1)
    before = lax.ppermute(last, axis, up)
    after = lax.ppermute(first, axis, down)
    return before, after


def local_terms(orbital_field, potential):
    across = orbital_field.shape[2]
    depth_cells = orbital_field.shape[3]
    padded = jnp.pad(orbital_field, ((0, 0), (0, 0), (6, 6), (6, 6)))
    total = 3.0 * coefs[0] * orbital_field
    for k in range(1, 7):
        total = total + coefs[k] * (
            padded[:, :, 6 + k : 6 + k + across, 6 : 6 + depth_cells]
            + padded[:, :, 6 - k : 6 - k + across, 6 : 6 + depth_cells]
        )
        total = total + coefs[k] * (
            padded[:, :, 6 : 6 + across, 6 + k : 6 + k + depth_cells]
            + padded[:, :, 6 : 6 + across, 6 - k : 6 - k + depth_cells]
        )
    return -2.0 * total + potential[None] * orbital_field


def combine_kernel(scale, with_base, *refs):
    if with_base:
        local_ref, own_ref, before_ref, after_ref, base_ref, out_ref = refs
    else:
        local_ref, own_ref, before_ref, after_ref, out_ref = refs
    width = before_ref.shape[1]
    planes_own = own_ref.shape[1]

    def plane(q):
        if q < 0:
            return before_ref[:, width + q]
        if q >= planes_own:
            return after_ref[:, q - planes_own]
        return own_ref[:, q]

    for p in range(planes_own):
        acc = coefs[1] * (plane(p + 1) + plane(p - 1))
        for k in range(2, 7):
            acc = acc + coefs[k] * (plane(p + k) + plane(p - k))
        value = local_ref[:, p] - 2.0 * acc
        value = scale * (value - centre * own_ref[:, p]) / radius
        if with_base:
            value = value - base_ref[:, p]
        out_ref[:, p] = value


def filter_step(
    local, orbital_field, before, after, scale, base=None, start=0, count=None, base_start=0, halo_start=None
):
    count = orbital_field.shape[0] if count is None else count
    halo_start = start if halo_start is None else halo_start
    aligned = all(value % 8 == 0 for value in (count, start, base_start, halo_start))
    block_rows = 8 if aligned else 1
    offset = start // block_rows
    halo_offset = halo_start // block_rows
    base_offset = base_start // block_rows
    block = (block_rows,) + orbital_field.shape[1:]
    halo_block = (block_rows,) + before.shape[1:]
    spec = pl.BlockSpec(block, lambda i: (i + offset, 0, 0, 0))
    halo_spec = pl.BlockSpec(halo_block, lambda i: (i + halo_offset, 0, 0, 0))
    operands = [local, orbital_field, before, after]
    specs = [spec, spec, halo_spec, halo_spec]
    if base is not None:
        operands.append(base)
        specs.append(pl.BlockSpec(block, lambda i: (i + base_offset, 0, 0, 0)))
    return pl.pallas_call(
        functools.partial(combine_kernel, scale, base is not None),
        grid=(count // block_rows,),
        in_specs=specs,
        out_specs=pl.BlockSpec(block, lambda i: (i, 0, 0, 0)),
        out_shape=jax.ShapeDtypeStruct((count,) + orbital_field.shape[1:], jnp.float32),
    )(*operands)


def copy_kernel(source_ref, result_ref):
    result_ref[...] = source_ref[...]


def take_rows(value, start, count):
    block_rows = 8 if count % 8 == 0 and start % 8 == 0 else 1
    offset = start // block_rows
    block = (block_rows,) + value.shape[1:]
    return pl.pallas_call(
        copy_kernel,
        grid=(count // block_rows,),
        in_specs=[pl.BlockSpec(block, lambda i: (i + offset, 0, 0, 0))],
        out_specs=pl.BlockSpec(block, lambda i: (i, 0, 0, 0)),
        out_shape=jax.ShapeDtypeStruct((count,) + value.shape[1:], value.dtype),
    )(value)


def spread_cells(filtered):
    rows = filtered.shape[0]
    parts = lax.axis_size("orb")
    lanes = filtered.shape[3]
    rows_per_part = filtered.shape[1] * filtered.shape[2] // parts
    chunks = filtered.reshape(rows, parts, rows_per_part, lanes)
    return lax.all_to_all(chunks, "orb", 1, 0, tiled=True).reshape(parts, rows, rows_per_part, lanes)


def gram_matrix(left_rows, right_rows):
    return lax.dot_general(
        left_rows,
        right_rows,
        (((1, 2), (1, 2)), ((), ())),
        precision=matmul_precision,
        preferred_element_type=jnp.float32,
    )


def apply_rows(inverse, source_rows):
    return lax.dot_general(
        inverse,
        source_rows,
        (((0,), (0,)), ((), ())),
        precision=matmul_precision,
        preferred_element_type=jnp.float32,
    )


def mix_rows(weights, source_rows):
    return lax.dot_general(
        weights,
        source_rows,
        (((1,), (0,)), ((), ())),
        precision=matmul_precision,
        preferred_element_type=jnp.float32,
    )


def group_round(value, axis, stride, radix):
    size = lax.axis_size(axis)
    position = (lax.axis_index(axis) // stride) % radix
    received = [value]
    for shift in range(1, radix):
        pairs = []
        for i in range(size):
            p = (i // stride) % radix
            pairs.append((i, i + ((p + shift) % radix - p) * stride))
        received.append(lax.ppermute(value, axis, pairs))
    total = None
    for q in range(radix):
        choice = (position - q) % radix
        term = received[0]
        for shift in range(1, radix):
            term = jnp.where(choice == shift, received[shift], term)
        total = term if total is None else total + term
    return total


def exchange_sum(value, axis):
    size = lax.axis_size(axis)
    if size & (size - 1):
        return lax.psum(value, axis)
    stride = 1
    if size.bit_length() % 2 == 0:
        value = group_round(value, axis, 1, 2)
        stride = 2
    while stride < size:
        value = group_round(value, axis, stride, 4)
        stride *= 4
    return value


def cell_sum(value):
    return exchange_sum(exchange_sum(value, "grid"), "orb")


def eliminate_kernel(source_ref, result_ref):
    result_ref[...] = source_ref[...]
    rows, width = result_ref.shape
    lanes = lax.broadcasted_iota(jnp.int32, (1, width), 1)
    cols = lax.broadcasted_iota(jnp.int32, (rows, width), 1)
    row_ids = lax.broadcasted_iota(jnp.int32, (rows, 1), 0)

    def column_step(column, carry):
        current = result_ref[pl.ds(column, 1), :]
        pivot_value = jnp.sum(jnp.where(lanes == column, current, 0.0), axis=1, keepdims=True)
        inv_root = 1.0 / jnp.sqrt(pivot_value)
        scaled = jnp.where(lanes >= column, current, 0.0) * inv_root
        whole = result_ref[...]
        below = jnp.sum(jnp.where(cols == column, whole, 0.0), axis=1, keepdims=True) * inv_root
        below = jnp.where(row_ids > column, below, 0.0)
        whole = whole - below * scaled
        result_ref[...] = jnp.where(row_ids == column, scaled, whole)
        return carry

    lax.fori_loop(0, rows, column_step, 0)


def eliminate(matrix, extra):
    source = jnp.concatenate([matrix, extra], axis=1)
    return pl.pallas_call(
        eliminate_kernel,
        out_shape=jax.ShapeDtypeStruct(source.shape, jnp.float32),
    )(source)


def factorize(rows_block, inv_cells):
    panel_rows = rows_block.shape[0] // 2
    leading = cell_sum(gram_matrix(rows_block[:panel_rows], rows_block)) * inv_cells
    eye = jnp.eye(panel_rows, dtype=jnp.float32)
    first = eliminate(leading, eye)
    first_r = first[:, :panel_rows]
    coupling = first[:, panel_rows : 2 * panel_rows]
    first_lower_inv = first[:, 2 * panel_rows :]
    first_q = mix_rows(first_lower_inv, rows_block[:panel_rows])
    remainder = rows_block[panel_rows:] - apply_rows(coupling, first_q)
    trailing = cell_sum(gram_matrix(remainder, remainder)) * inv_cells
    second = eliminate(trailing, eye)
    second_r = second[:, :panel_rows]
    second_lower_inv = second[:, panel_rows:]
    upper_rows = jnp.concatenate([first_r, coupling], axis=1)
    lower_rows = jnp.concatenate(
        [jnp.zeros((second_r.shape[0], panel_rows), jnp.float32), second_r], axis=1
    )
    triangle = jnp.concatenate([upper_rows, lower_rows], axis=0)
    return triangle, first_q, second_lower_inv, remainder


def local(orbital_block, potential):
    orb_rows = orbital_block.shape[0]
    half = orb_rows // 2
    local_part = local_terms(orbital_block, potential)
    before_0, after_0 = halo_planes(take_rows(orbital_block, 0, half), "grid", 6)
    local_part, before_0, after_0 = lax.optimization_barrier((local_part, before_0, after_0))
    second_rows, before_0, after_0 = lax.optimization_barrier((take_rows(orbital_block, half, orb_rows - half), before_0, after_0))
    before_1, after_1 = halo_planes(second_rows, "grid", 6)
    first_a = filter_step(local_part, orbital_block, before_0, after_0, 1.0, start=0, count=half)
    before_1, after_1 = lax.optimization_barrier((before_1, after_1))
    first_b = filter_step(
        local_part, orbital_block, before_1, after_1, 1.0, start=half, count=orb_rows - half, halo_start=0
    )
    before_a, after_a = halo_planes(first_a, "grid", 6)
    local_a = local_terms(first_a, potential)
    local_a, before_a, after_a, first_b = lax.optimization_barrier((local_a, before_a, after_a, first_b))
    before_b, after_b = halo_planes(first_b, "grid", 6)
    filtered_a = filter_step(local_a, first_a, before_a, after_a, 2.0, base=orbital_block)
    spread_a = spread_cells(filtered_a)
    local_b = local_terms(first_b, potential)
    local_b, before_b, after_b = lax.optimization_barrier((local_b, before_b, after_b))
    filtered_b = lax.optimization_barrier(
        filter_step(local_b, first_b, before_b, after_b, 2.0, base=orbital_block, base_start=half)
    )
    spread_b = spread_cells(filtered_b)
    parts, _, rows_per_part, lanes = spread_a.shape
    spread = jnp.stack([spread_a, spread_b], axis=1).reshape(-1, rows_per_part, lanes)
    inv_cells = 1.0 / (lax.axis_size("grid") * parts * rows_per_part * lanes)
    triangle, first_q, second_lower_inv, remainder = factorize(spread, inv_cells)
    second_q = mix_rows(second_lower_inv, remainder)
    orbitals = jnp.concatenate([first_q, second_q], axis=0)
    orbitals = orbitals.reshape(orbitals.shape[0], 1, rows_per_part, lanes)
    orbitals = lax.all_to_all(orbitals, "orb", 0, 1, tiled=True)
    return (orbitals.reshape(orbital_block.shape), triangle)


def solution(mesh):
    in_specs = (P("orb", "grid", None, None), P("grid", None, None))
    out_specs = (P("orb", "grid", None, None), P())
    return jax.shard_map(local, mesh=mesh, in_specs=in_specs, out_specs=out_specs, check_vma=False)
```

```python
import functools

import jax
import jax.numpy as jnp
from jax import lax
from jax.experimental import pallas as pl
from jax.experimental.pallas import tpu as pltpu
from jax.sharding import PartitionSpec as P

coefs = (
    -5369.0 / 1800.0,
    12.0 / 7.0,
    -15.0 / 56.0,
    10.0 / 189.0,
    -1.0 / 112.0,
    2.0 / 1925.0,
    -1.0 / 16632.0,
)
centre = 23.5
radius = 19.5
matmul_precision = lax.Precision.HIGH


def halo_planes(value, axis, width):
    size, length = (lax.axis_size(axis), value.shape[1])
    up = [(i, (i + 1) % size) for i in range(size - 1)]
    down = [(j, i) for i, j in up]
    last = lax.slice_in_dim(value, length - width, length, axis=1)
    first = lax.slice_in_dim(value, 0, width, axis=1)
    before = lax.ppermute(last, axis, up)
    after = lax.ppermute(first, axis, down)
    return before, after


def local_terms(orbital_field, potential):
    across = orbital_field.shape[2]
    depth_cells = orbital_field.shape[3]
    padded = jnp.pad(orbital_field, ((0, 0), (0, 0), (6, 6), (6, 6)))
    total = 3.0 * coefs[0] * orbital_field
    for k in range(1, 7):
        total = total + coefs[k] * (
            padded[:, :, 6 + k : 6 + k + across, 6 : 6 + depth_cells]
            + padded[:, :, 6 - k : 6 - k + across, 6 : 6 + depth_cells]
        )
        total = total + coefs[k] * (
            padded[:, :, 6 : 6 + across, 6 + k : 6 + k + depth_cells]
            + padded[:, :, 6 : 6 + across, 6 - k : 6 - k + depth_cells]
        )
    return -2.0 * total + potential[None] * orbital_field


def combine_kernel(scale, with_base, *refs):
    if with_base:
        local_ref, own_ref, before_ref, after_ref, base_ref, out_ref = refs
    else:
        local_ref, own_ref, before_ref, after_ref, out_ref = refs
    width = before_ref.shape[1]
    planes_own = own_ref.shape[1]

    def plane(q):
        if q < 0:
            return before_ref[:, width + q]
        if q >= planes_own:
            return after_ref[:, q - planes_own]
        return own_ref[:, q]

    for p in range(planes_own):
        acc = coefs[1] * (plane(p + 1) + plane(p - 1))
        for k in range(2, 7):
            acc = acc + coefs[k] * (plane(p + k) + plane(p - k))
        value = local_ref[:, p] - 2.0 * acc
        value = scale * (value - centre * own_ref[:, p]) / radius
        if with_base:
            value = value - base_ref[:, p]
        out_ref[:, p] = value


def filter_step(
    local, orbital_field, before, after, scale, base=None, start=0, count=None, base_start=0, halo_start=None
):
    count = orbital_field.shape[0] if count is None else count
    halo_start = start if halo_start is None else halo_start
    aligned = all(value % 8 == 0 for value in (count, start, base_start, halo_start))
    block_rows = 8 if aligned else 1
    offset = start // block_rows
    halo_offset = halo_start // block_rows
    base_offset = base_start // block_rows
    block = (block_rows,) + orbital_field.shape[1:]
    halo_block = (block_rows,) + before.shape[1:]
    spec = pl.BlockSpec(block, lambda i: (i + offset, 0, 0, 0))
    halo_spec = pl.BlockSpec(halo_block, lambda i: (i + halo_offset, 0, 0, 0))
    operands = [local, orbital_field, before, after]
    specs = [spec, spec, halo_spec, halo_spec]
    if base is not None:
        operands.append(base)
        specs.append(pl.BlockSpec(block, lambda i: (i + base_offset, 0, 0, 0)))
    return pl.pallas_call(
        functools.partial(combine_kernel, scale, base is not None),
        grid=(count // block_rows,),
        in_specs=specs,
        out_specs=pl.BlockSpec(block, lambda i: (i, 0, 0, 0)),
        out_shape=jax.ShapeDtypeStruct((count,) + orbital_field.shape[1:], jnp.float32),
    )(*operands)


def spread_cells(filtered):
    rows = filtered.shape[0]
    parts = lax.axis_size("orb")
    lanes = filtered.shape[3]
    rows_per_part = filtered.shape[1] * filtered.shape[2] // parts
    chunks = filtered.reshape(rows, parts, rows_per_part, lanes)
    return lax.all_to_all(chunks, "orb", 1, 0, tiled=True).reshape(parts, rows, rows_per_part, lanes)


def gram_matrix(left_rows, right_rows):
    return lax.dot_general(
        left_rows,
        right_rows,
        (((1, 2), (1, 2)), ((), ())),
        precision=matmul_precision,
        preferred_element_type=jnp.float32,
    )


def apply_rows(inverse, source_rows):
    return lax.dot_general(
        inverse,
        source_rows,
        (((0,), (0,)), ((), ())),
        precision=matmul_precision,
        preferred_element_type=jnp.float32,
    )


def mix_rows(weights, source_rows):
    return lax.dot_general(
        weights,
        source_rows,
        (((1,), (0,)), ((), ())),
        precision=matmul_precision,
        preferred_element_type=jnp.float32,
    )


def exchange_sum(value, axis):
    size = lax.axis_size(axis)
    if size & (size - 1):
        return lax.psum(value, axis)
    step = 1
    while step < size:
        value = value + lax.ppermute(value, axis, [(i, i ^ step) for i in range(size)])
        step *= 2
    return value


def cell_sum(value):
    return exchange_sum(exchange_sum(value, "grid"), "orb")


def eliminate_kernel(source_ref, result_ref):
    result_ref[...] = source_ref[...]
    rows, width = result_ref.shape
    lanes = lax.broadcasted_iota(jnp.int32, (1, width), 1)
    cols = lax.broadcasted_iota(jnp.int32, (rows, width), 1)
    row_ids = lax.broadcasted_iota(jnp.int32, (rows, 1), 0)

    def column_step(column, carry):
        current = result_ref[pl.ds(column, 1), :]
        pivot_value = jnp.sum(jnp.where(lanes == column, current, 0.0), axis=1, keepdims=True)
        inv_root = 1.0 / jnp.sqrt(pivot_value)
        scaled = jnp.where(lanes >= column, current, 0.0) * inv_root
        whole = result_ref[...]
        below = jnp.sum(jnp.where(cols == column, whole, 0.0), axis=1, keepdims=True) * inv_root
        below = jnp.where(row_ids > column, below, 0.0)
        whole = whole - below * scaled
        result_ref[...] = jnp.where(row_ids == column, scaled, whole)
        return carry

    lax.fori_loop(0, rows, column_step, 0)


def eliminate(matrix, extra):
    source = jnp.concatenate([matrix, extra], axis=1)
    return pl.pallas_call(
        eliminate_kernel,
        out_shape=jax.ShapeDtypeStruct(source.shape, jnp.float32),
    )(source)


def factorize(rows_block, inv_cells):
    panel_rows = rows_block.shape[0] // 2
    leading = cell_sum(gram_matrix(rows_block[:panel_rows], rows_block)) * inv_cells
    eye = jnp.eye(panel_rows, dtype=jnp.float32)
    first = eliminate(leading, eye)
    first_r = first[:, :panel_rows]
    coupling = first[:, panel_rows : 2 * panel_rows]
    first_lower_inv = first[:, 2 * panel_rows :]
    first_q = mix_rows(first_lower_inv, rows_block[:panel_rows])
    remainder = rows_block[panel_rows:] - apply_rows(coupling, first_q)
    trailing = cell_sum(gram_matrix(remainder, remainder)) * inv_cells
    second = eliminate(trailing, eye)
    second_r = second[:, :panel_rows]
    second_lower_inv = second[:, panel_rows:]
    upper_rows = jnp.concatenate([first_r, coupling], axis=1)
    lower_rows = jnp.concatenate(
        [jnp.zeros((second_r.shape[0], panel_rows), jnp.float32), second_r], axis=1
    )
    triangle = jnp.concatenate([upper_rows, lower_rows], axis=0)
    return triangle, first_q, second_lower_inv, remainder


def local(orbital_block, potential):
    orb_rows = orbital_block.shape[0]
    half = orb_rows // 2
    local_part = local_terms(orbital_block, potential)
    before_0, after_0 = halo_planes(orbital_block[:half], "grid", 6)
    local_part, before_0, after_0 = lax.optimization_barrier((local_part, before_0, after_0))
    second_rows, before_0, after_0 = lax.optimization_barrier((orbital_block[half:], before_0, after_0))
    before_1, after_1 = halo_planes(second_rows, "grid", 6)
    first_a = filter_step(local_part, orbital_block, before_0, after_0, 1.0, start=0, count=half)
    before_1, after_1 = lax.optimization_barrier((before_1, after_1))
    first_b = filter_step(
        local_part, orbital_block, before_1, after_1, 1.0, start=half, count=orb_rows - half, halo_start=0
    )
    before_a, after_a = halo_planes(first_a, "grid", 6)
    local_a = local_terms(first_a, potential)
    local_a, before_a, after_a, first_b = lax.optimization_barrier((local_a, before_a, after_a, first_b))
    before_b, after_b = halo_planes(first_b, "grid", 6)
    filtered_a = filter_step(local_a, first_a, before_a, after_a, 2.0, base=orbital_block)
    spread_a = spread_cells(filtered_a)
    local_b = local_terms(first_b, potential)
    local_b, before_b, after_b = lax.optimization_barrier((local_b, before_b, after_b))
    filtered_b = lax.optimization_barrier(
        filter_step(local_b, first_b, before_b, after_b, 2.0, base=orbital_block, base_start=half)
    )
    spread_b = spread_cells(filtered_b)
    parts, _, rows_per_part, lanes = spread_a.shape
    spread = jnp.stack([spread_a, spread_b], axis=1).reshape(-1, rows_per_part, lanes)
    inv_cells = 1.0 / (lax.axis_size("grid") * parts * rows_per_part * lanes)
    triangle, first_q, second_lower_inv, remainder = factorize(spread, inv_cells)
    second_q = mix_rows(second_lower_inv, remainder)
    orbitals = jnp.concatenate([first_q, second_q], axis=0)
    orbitals = orbitals.reshape(orbitals.shape[0], 1, rows_per_part, lanes)
    orbitals = lax.all_to_all(orbitals, "orb", 0, 1, tiled=True)
    return (orbitals.reshape(orbital_block.shape), triangle)


def solution(mesh):
    in_specs = (P("orb", "grid", None, None), P("grid", None, None))
    out_specs = (P("orb", "grid", None, None), P())
    return jax.shard_map(local, mesh=mesh, in_specs=in_specs, out_specs=out_specs, check_vma=False)
```

```python
import functools

import jax
import jax.numpy as jnp
from jax import lax
from jax.experimental import pallas as pl
from jax.experimental.pallas import tpu as pltpu
from jax.sharding import PartitionSpec as P

coefs = (
    -5369.0 / 1800.0,
    12.0 / 7.0,
    -15.0 / 56.0,
    10.0 / 189.0,
    -1.0 / 112.0,
    2.0 / 1925.0,
    -1.0 / 16632.0,
)
centre = 23.5
radius = 19.5
matmul_precision = lax.Precision.HIGH


def halo_planes(value, axis, width):
    size, length = (lax.axis_size(axis), value.shape[1])
    up = [(i, (i + 1) % size) for i in range(size - 1)]
    down = [(j, i) for i, j in up]
    last = lax.slice_in_dim(value, length - width, length, axis=1)
    first = lax.slice_in_dim(value, 0, width, axis=1)
    before = lax.ppermute(last, axis, up)
    after = lax.ppermute(first, axis, down)
    return before, after


def local_terms(orbital_field, potential):
    across = orbital_field.shape[2]
    depth_cells = orbital_field.shape[3]
    padded = jnp.pad(orbital_field, ((0, 0), (0, 0), (6, 6), (6, 6)))
    total = 3.0 * coefs[0] * orbital_field
    for k in range(1, 7):
        total = total + coefs[k] * (
            padded[:, :, 6 + k : 6 + k + across, 6 : 6 + depth_cells]
            + padded[:, :, 6 - k : 6 - k + across, 6 : 6 + depth_cells]
        )
        total = total + coefs[k] * (
            padded[:, :, 6 : 6 + across, 6 + k : 6 + k + depth_cells]
            + padded[:, :, 6 : 6 + across, 6 - k : 6 - k + depth_cells]
        )
    return -2.0 * total + potential[None] * orbital_field


def combine_kernel(scale, with_base, *refs):
    if with_base:
        local_ref, own_ref, before_ref, after_ref, base_ref, out_ref = refs
    else:
        local_ref, own_ref, before_ref, after_ref, out_ref = refs
    width = before_ref.shape[1]
    planes_own = own_ref.shape[1]

    def plane(q):
        if q < 0:
            return before_ref[:, width + q]
        if q >= planes_own:
            return after_ref[:, q - planes_own]
        return own_ref[:, q]

    for p in range(planes_own):
        acc = coefs[1] * (plane(p + 1) + plane(p - 1))
        for k in range(2, 7):
            acc = acc + coefs[k] * (plane(p + k) + plane(p - k))
        value = local_ref[:, p] - 2.0 * acc
        value = scale * (value - centre * own_ref[:, p]) / radius
        if with_base:
            value = value - base_ref[:, p]
        out_ref[:, p] = value


def filter_step(
    local, orbital_field, before, after, scale, base=None, start=0, count=None, base_start=0, halo_start=None
):
    count = orbital_field.shape[0] if count is None else count
    halo_start = start if halo_start is None else halo_start
    aligned = all(value % 4 == 0 for value in (count, start, base_start, halo_start))
    block_rows = 4 if aligned else 1
    offset = start // block_rows
    halo_offset = halo_start // block_rows
    base_offset = base_start // block_rows
    block = (block_rows,) + orbital_field.shape[1:]
    halo_block = (block_rows,) + before.shape[1:]
    spec = pl.BlockSpec(block, lambda i: (i + offset, 0, 0, 0))
    halo_spec = pl.BlockSpec(halo_block, lambda i: (i + halo_offset, 0, 0, 0))
    operands = [local, orbital_field, before, after]
    specs = [spec, spec, halo_spec, halo_spec]
    if base is not None:
        operands.append(base)
        specs.append(pl.BlockSpec(block, lambda i: (i + base_offset, 0, 0, 0)))
    return pl.pallas_call(
        functools.partial(combine_kernel, scale, base is not None),
        grid=(count // block_rows,),
        in_specs=specs,
        out_specs=pl.BlockSpec(block, lambda i: (i, 0, 0, 0)),
        out_shape=jax.ShapeDtypeStruct((count,) + orbital_field.shape[1:], jnp.float32),
    )(*operands)


def spread_cells(filtered):
    rows = filtered.shape[0]
    parts = lax.axis_size("orb")
    lanes = filtered.shape[3]
    rows_per_part = filtered.shape[1] * filtered.shape[2] // parts
    chunks = filtered.reshape(rows, parts, rows_per_part, lanes)
    return lax.all_to_all(chunks, "orb", 1, 0, tiled=True).reshape(parts, rows, rows_per_part, lanes)


def gram_matrix(left_rows, right_rows):
    return lax.dot_general(
        left_rows,
        right_rows,
        (((1, 2), (1, 2)), ((), ())),
        precision=matmul_precision,
        preferred_element_type=jnp.float32,
    )


def apply_rows(inverse, source_rows):
    return lax.dot_general(
        inverse,
        source_rows,
        (((0,), (0,)), ((), ())),
        precision=matmul_precision,
        preferred_element_type=jnp.float32,
    )


def mix_rows(weights, source_rows):
    return lax.dot_general(
        weights,
        source_rows,
        (((1,), (0,)), ((), ())),
        precision=matmul_precision,
        preferred_element_type=jnp.float32,
    )


def group_round(value, axis, stride, radix):
    size = lax.axis_size(axis)
    position = (lax.axis_index(axis) // stride) % radix
    received = [value]
    for shift in range(1, radix):
        pairs = []
        for i in range(size):
            p = (i // stride) % radix
            pairs.append((i, i + ((p + shift) % radix - p) * stride))
        received.append(lax.ppermute(value, axis, pairs))
    total = None
    for q in range(radix):
        choice = (position - q) % radix
        term = received[0]
        for shift in range(1, radix):
            term = jnp.where(choice == shift, received[shift], term)
        total = term if total is None else total + term
    return total


def exchange_sum(value, axis):
    size = lax.axis_size(axis)
    if size & (size - 1):
        return lax.psum(value, axis)
    stride = 1
    if size.bit_length() % 2 == 0:
        value = group_round(value, axis, 1, 2)
        stride = 2
    while stride < size:
        value = group_round(value, axis, stride, 4)
        stride *= 4
    return value


def cell_sum(value):
    return exchange_sum(exchange_sum(value, "grid"), "orb")


def eliminate_kernel(source_ref, result_ref):
    result_ref[...] = source_ref[...]
    rows, width = result_ref.shape
    lanes = lax.broadcasted_iota(jnp.int32, (1, width), 1)
    cols = lax.broadcasted_iota(jnp.int32, (rows, width), 1)
    row_ids = lax.broadcasted_iota(jnp.int32, (rows, 1), 0)

    def column_step(column, carry):
        current = result_ref[pl.ds(column, 1), :]
        pivot_value = jnp.sum(jnp.where(lanes == column, current, 0.0), axis=1, keepdims=True)
        inv_root = 1.0 / jnp.sqrt(pivot_value)
        scaled = jnp.where(lanes >= column, current, 0.0) * inv_root
        whole = result_ref[...]
        below = jnp.sum(jnp.where(cols == column, whole, 0.0), axis=1, keepdims=True) * inv_root
        below = jnp.where(row_ids > column, below, 0.0)
        whole = whole - below * scaled
        result_ref[...] = jnp.where(row_ids == column, scaled, whole)
        return carry

    lax.fori_loop(0, rows, column_step, 0)


def eliminate(matrix, extra):
    source = jnp.concatenate([matrix, extra], axis=1)
    return pl.pallas_call(
        eliminate_kernel,
        out_shape=jax.ShapeDtypeStruct(source.shape, jnp.float32),
    )(source)


def factorize(rows_block, inv_cells):
    panel_rows = rows_block.shape[0] // 2
    leading = cell_sum(gram_matrix(rows_block[:panel_rows], rows_block)) * inv_cells
    eye = jnp.eye(panel_rows, dtype=jnp.float32)
    first = eliminate(leading, eye)
    first_r = first[:, :panel_rows]
    coupling = first[:, panel_rows : 2 * panel_rows]
    first_lower_inv = first[:, 2 * panel_rows :]
    first_q = mix_rows(first_lower_inv, rows_block[:panel_rows])
    remainder = rows_block[panel_rows:] - apply_rows(coupling, first_q)
    trailing = cell_sum(gram_matrix(remainder, remainder)) * inv_cells
    second = eliminate(trailing, eye)
    second_r = second[:, :panel_rows]
    second_lower_inv = second[:, panel_rows:]
    upper_rows = jnp.concatenate([first_r, coupling], axis=1)
    lower_rows = jnp.concatenate(
        [jnp.zeros((second_r.shape[0], panel_rows), jnp.float32), second_r], axis=1
    )
    triangle = jnp.concatenate([upper_rows, lower_rows], axis=0)
    return triangle, first_q, second_lower_inv, remainder


def local(orbital_block, potential):
    orb_rows = orbital_block.shape[0]
    half = orb_rows // 2
    local_part = local_terms(orbital_block, potential)
    before_0, after_0 = halo_planes(orbital_block[:half], "grid", 6)
    local_part, before_0, after_0 = lax.optimization_barrier((local_part, before_0, after_0))
    second_rows, before_0, after_0 = lax.optimization_barrier((orbital_block[half:], before_0, after_0))
    before_1, after_1 = halo_planes(second_rows, "grid", 6)
    first_a = filter_step(local_part, orbital_block, before_0, after_0, 1.0, start=0, count=half)
    before_1, after_1 = lax.optimization_barrier((before_1, after_1))
    first_b = filter_step(
        local_part, orbital_block, before_1, after_1, 1.0, start=half, count=orb_rows - half, halo_start=0
    )
    before_a, after_a = halo_planes(first_a, "grid", 6)
    local_a = local_terms(first_a, potential)
    local_a, before_a, after_a, first_b = lax.optimization_barrier((local_a, before_a, after_a, first_b))
    before_b, after_b = halo_planes(first_b, "grid", 6)
    filtered_a = filter_step(local_a, first_a, before_a, after_a, 2.0, base=orbital_block)
    spread_a = spread_cells(filtered_a)
    local_b = local_terms(first_b, potential)
    local_b, before_b, after_b = lax.optimization_barrier((local_b, before_b, after_b))
    filtered_b = lax.optimization_barrier(
        filter_step(local_b, first_b, before_b, after_b, 2.0, base=orbital_block, base_start=half)
    )
    spread_b = spread_cells(filtered_b)
    parts, _, rows_per_part, lanes = spread_a.shape
    spread = jnp.stack([spread_a, spread_b], axis=1).reshape(-1, rows_per_part, lanes)
    inv_cells = 1.0 / (lax.axis_size("grid") * parts * rows_per_part * lanes)
    triangle, first_q, second_lower_inv, remainder = factorize(spread, inv_cells)
    second_q = mix_rows(second_lower_inv, remainder)
    orbitals = jnp.concatenate([first_q, second_q], axis=0)
    orbitals = orbitals.reshape(orbitals.shape[0], 1, rows_per_part, lanes)
    orbitals = lax.all_to_all(orbitals, "orb", 0, 1, tiled=True)
    return (orbitals.reshape(orbital_block.shape), triangle)


def solution(mesh):
    in_specs = (P("orb", "grid", None, None), P("grid", None, None))
    out_specs = (P("orb", "grid", None, None), P())
    return jax.shard_map(local, mesh=mesh, in_specs=in_specs, out_specs=out_specs, check_vma=False)
```

```python
import functools

import jax
import jax.numpy as jnp
from jax import lax
from jax.experimental import pallas as pl
from jax.experimental.pallas import tpu as pltpu
from jax.sharding import PartitionSpec as P

coefs = (
    -5369.0 / 1800.0,
    12.0 / 7.0,
    -15.0 / 56.0,
    10.0 / 189.0,
    -1.0 / 112.0,
    2.0 / 1925.0,
    -1.0 / 16632.0,
)
centre = 23.5
radius = 19.5
matmul_precision = lax.Precision.HIGH


def halo_planes(value, axis, width):
    size, length = (lax.axis_size(axis), value.shape[1])
    up = [(i, (i + 1) % size) for i in range(size - 1)]
    down = [(j, i) for i, j in up]
    last = lax.slice_in_dim(value, length - width, length, axis=1)
    first = lax.slice_in_dim(value, 0, width, axis=1)
    before = lax.ppermute(last, axis, up)
    after = lax.ppermute(first, axis, down)
    return before, after


def local_terms(orbital_field, potential):
    across = orbital_field.shape[2]
    depth_cells = orbital_field.shape[3]
    padded = jnp.pad(orbital_field, ((0, 0), (0, 0), (6, 6), (6, 6)))
    total = 3.0 * coefs[0] * orbital_field
    for k in range(1, 7):
        total = total + coefs[k] * (
            padded[:, :, 6 + k : 6 + k + across, 6 : 6 + depth_cells]
            + padded[:, :, 6 - k : 6 - k + across, 6 : 6 + depth_cells]
        )
        total = total + coefs[k] * (
            padded[:, :, 6 : 6 + across, 6 + k : 6 + k + depth_cells]
            + padded[:, :, 6 : 6 + across, 6 - k : 6 - k + depth_cells]
        )
    return -2.0 * total + potential[None] * orbital_field


def combine_kernel(scale, with_base, *refs):
    if with_base:
        local_ref, own_ref, before_ref, after_ref, base_ref, out_ref = refs
    else:
        local_ref, own_ref, before_ref, after_ref, out_ref = refs
    width = before_ref.shape[1]
    planes_own = own_ref.shape[1]

    def plane(q):
        if q < 0:
            return before_ref[:, width + q]
        if q >= planes_own:
            return after_ref[:, q - planes_own]
        return own_ref[:, q]

    for p in range(planes_own):
        acc = coefs[1] * (plane(p + 1) + plane(p - 1))
        for k in range(2, 7):
            acc = acc + coefs[k] * (plane(p + k) + plane(p - k))
        value = local_ref[:, p] - 2.0 * acc
        value = scale * (value - centre * own_ref[:, p]) / radius
        if with_base:
            value = value - base_ref[:, p]
        out_ref[:, p] = value


def filter_step(
    local, orbital_field, before, after, scale, base=None, start=0, count=None, base_start=0, halo_start=None
):
    count = orbital_field.shape[0] if count is None else count
    halo_start = start if halo_start is None else halo_start
    aligned = all(value % 8 == 0 for value in (count, start, base_start, halo_start))
    block_rows = 8 if aligned else 1
    offset = start // block_rows
    halo_offset = halo_start // block_rows
    base_offset = base_start // block_rows
    block = (block_rows,) + orbital_field.shape[1:]
    halo_block = (block_rows,) + before.shape[1:]
    spec = pl.BlockSpec(block, lambda i: (i + offset, 0, 0, 0))
    halo_spec = pl.BlockSpec(halo_block, lambda i: (i + halo_offset, 0, 0, 0))
    operands = [local, orbital_field, before, after]
    specs = [spec, spec, halo_spec, halo_spec]
    if base is not None:
        operands.append(base)
        specs.append(pl.BlockSpec(block, lambda i: (i + base_offset, 0, 0, 0)))
    return pl.pallas_call(
        functools.partial(combine_kernel, scale, base is not None),
        grid=(count // block_rows,),
        in_specs=specs,
        out_specs=pl.BlockSpec(block, lambda i: (i, 0, 0, 0)),
        out_shape=jax.ShapeDtypeStruct((count,) + orbital_field.shape[1:], jnp.float32),
    )(*operands)


def spread_cells(filtered):
    rows = filtered.shape[0]
    parts = lax.axis_size("orb")
    lanes = filtered.shape[3]
    rows_per_part = filtered.shape[1] * filtered.shape[2] // parts
    chunks = filtered.reshape(rows, parts, rows_per_part, lanes)
    return lax.all_to_all(chunks, "orb", 1, 0, tiled=True).reshape(parts, rows, rows_per_part, lanes)


def gram_matrix(left_rows, right_rows):
    return lax.dot_general(
        left_rows,
        right_rows,
        (((1, 2), (1, 2)), ((), ())),
        precision=matmul_precision,
        preferred_element_type=jnp.float32,
    )


def apply_rows(inverse, source_rows):
    return lax.dot_general(
        inverse,
        source_rows,
        (((0,), (0,)), ((), ())),
        precision=matmul_precision,
        preferred_element_type=jnp.float32,
    )


def mix_rows(weights, source_rows):
    return lax.dot_general(
        weights,
        source_rows,
        (((1,), (0,)), ((), ())),
        precision=matmul_precision,
        preferred_element_type=jnp.float32,
    )


def group_round(value, axis, stride, radix):
    size = lax.axis_size(axis)
    position = (lax.axis_index(axis) // stride) % radix
    received = [value]
    for shift in range(1, radix):
        pairs = []
        for i in range(size):
            p = (i // stride) % radix
            pairs.append((i, i + ((p + shift) % radix - p) * stride))
        received.append(lax.ppermute(value, axis, pairs))
    total = None
    for q in range(radix):
        choice = (position - q) % radix
        term = received[0]
        for shift in range(1, radix):
            term = jnp.where(choice == shift, received[shift], term)
        total = term if total is None else total + term
    return total


def exchange_sum(value, axis):
    size = lax.axis_size(axis)
    if size & (size - 1):
        return lax.psum(value, axis)
    stride = 1
    if size.bit_length() % 2 == 0:
        value = group_round(value, axis, 1, 2)
        stride = 2
    while stride < size:
        value = group_round(value, axis, stride, 4)
        stride *= 4
    return value


def cell_sum(value):
    return exchange_sum(exchange_sum(value, "grid"), "orb")


def eliminate_kernel(source_ref, result_ref):
    result_ref[...] = source_ref[...]
    rows, width = result_ref.shape
    lanes = lax.broadcasted_iota(jnp.int32, (1, width), 1)
    cols = lax.broadcasted_iota(jnp.int32, (rows, width), 1)
    row_ids = lax.broadcasted_iota(jnp.int32, (rows, 1), 0)

    def column_step(column, carry):
        current = result_ref[pl.ds(column, 1), :]
        pivot_value = jnp.sum(jnp.where(lanes == column, current, 0.0), axis=1, keepdims=True)
        inv_root = lax.rsqrt(pivot_value)
        scaled = jnp.where(lanes >= column, current, 0.0) * inv_root
        whole = result_ref[...]
        below = jnp.sum(jnp.where(cols == column, whole, 0.0), axis=1, keepdims=True) * inv_root
        below = jnp.where(row_ids > column, below, 0.0)
        whole = whole - below * scaled
        result_ref[...] = jnp.where(row_ids == column, scaled, whole)
        return carry

    lax.fori_loop(0, rows, column_step, 0)


def eliminate(matrix, extra):
    source = jnp.concatenate([matrix, extra], axis=1)
    return pl.pallas_call(
        eliminate_kernel,
        out_shape=jax.ShapeDtypeStruct(source.shape, jnp.float32),
    )(source)


def factorize(rows_block, inv_cells):
    panel_rows = rows_block.shape[0] // 2
    leading = cell_sum(gram_matrix(rows_block[:panel_rows], rows_block)) * inv_cells
    eye = jnp.eye(panel_rows, dtype=jnp.float32)
    first = eliminate(leading, eye)
    first_r = first[:, :panel_rows]
    coupling = first[:, panel_rows : 2 * panel_rows]
    first_lower_inv = first[:, 2 * panel_rows :]
    first_q = mix_rows(first_lower_inv, rows_block[:panel_rows])
    remainder = rows_block[panel_rows:] - apply_rows(coupling, first_q)
    trailing = cell_sum(gram_matrix(remainder, remainder)) * inv_cells
    second = eliminate(trailing, eye)
    second_r = second[:, :panel_rows]
    second_lower_inv = second[:, panel_rows:]
    upper_rows = jnp.concatenate([first_r, coupling], axis=1)
    lower_rows = jnp.concatenate(
        [jnp.zeros((second_r.shape[0], panel_rows), jnp.float32), second_r], axis=1
    )
    triangle = jnp.concatenate([upper_rows, lower_rows], axis=0)
    return triangle, first_q, second_lower_inv, remainder


def local(orbital_block, potential):
    orb_rows = orbital_block.shape[0]
    half = orb_rows // 2
    local_part = local_terms(orbital_block, potential)
    before_0, after_0 = halo_planes(orbital_block[:half], "grid", 6)
    local_part, before_0, after_0 = lax.optimization_barrier((local_part, before_0, after_0))
    second_rows, before_0, after_0 = lax.optimization_barrier((orbital_block[half:], before_0, after_0))
    before_1, after_1 = halo_planes(second_rows, "grid", 6)
    first_a = filter_step(local_part, orbital_block, before_0, after_0, 1.0, start=0, count=half)
    before_1, after_1 = lax.optimization_barrier((before_1, after_1))
    first_b = filter_step(
        local_part, orbital_block, before_1, after_1, 1.0, start=half, count=orb_rows - half, halo_start=0
    )
    before_a, after_a = halo_planes(first_a, "grid", 6)
    local_a = local_terms(first_a, potential)
    local_a, before_a, after_a, first_b = lax.optimization_barrier((local_a, before_a, after_a, first_b))
    before_b, after_b = halo_planes(first_b, "grid", 6)
    filtered_a = filter_step(local_a, first_a, before_a, after_a, 2.0, base=orbital_block)
    spread_a = spread_cells(filtered_a)
    local_b = local_terms(first_b, potential)
    local_b, before_b, after_b = lax.optimization_barrier((local_b, before_b, after_b))
    filtered_b = lax.optimization_barrier(
        filter_step(local_b, first_b, before_b, after_b, 2.0, base=orbital_block, base_start=half)
    )
    spread_b = spread_cells(filtered_b)
    parts, _, rows_per_part, lanes = spread_a.shape
    spread = jnp.stack([spread_a, spread_b], axis=1).reshape(-1, rows_per_part, lanes)
    inv_cells = 1.0 / (lax.axis_size("grid") * parts * rows_per_part * lanes)
    triangle, first_q, second_lower_inv, remainder = factorize(spread, inv_cells)
    second_q = mix_rows(second_lower_inv, remainder)
    orbitals = jnp.concatenate([first_q, second_q], axis=0)
    orbitals = orbitals.reshape(orbitals.shape[0], 1, rows_per_part, lanes)
    orbitals = lax.all_to_all(orbitals, "orb", 0, 1, tiled=True)
    return (orbitals.reshape(orbital_block.shape), triangle)


def solution(mesh):
    in_specs = (P("orb", "grid", None, None), P("grid", None, None))
    out_specs = (P("orb", "grid", None, None), P())
    return jax.shard_map(local, mesh=mesh, in_specs=in_specs, out_specs=out_specs, check_vma=False)
```

```python
import functools

import jax
import jax.numpy as jnp
from jax import lax
from jax.experimental import pallas as pl
from jax.experimental.pallas import tpu as pltpu
from jax.sharding import PartitionSpec as P

coefs = (
    -5369.0 / 1800.0,
    12.0 / 7.0,
    -15.0 / 56.0,
    10.0 / 189.0,
    -1.0 / 112.0,
    2.0 / 1925.0,
    -1.0 / 16632.0,
)
centre = 23.5
radius = 19.5
matmul_precision = lax.Precision.HIGH


def halo_planes(value, axis, width):
    size, length = (lax.axis_size(axis), value.shape[1])
    up = [(i, (i + 1) % size) for i in range(size - 1)]
    down = [(j, i) for i, j in up]
    last = lax.slice_in_dim(value, length - width, length, axis=1)
    first = lax.slice_in_dim(value, 0, width, axis=1)
    before = lax.ppermute(last, axis, up)
    after = lax.ppermute(first, axis, down)
    return before, after


def local_terms(orbital_field, potential):
    across = orbital_field.shape[2]
    depth_cells = orbital_field.shape[3]
    padded = jnp.pad(orbital_field, ((0, 0), (0, 0), (6, 6), (6, 6)))
    total = 3.0 * coefs[0] * orbital_field
    for k in range(1, 7):
        total = total + coefs[k] * (
            padded[:, :, 6 + k : 6 + k + across, 6 : 6 + depth_cells]
            + padded[:, :, 6 - k : 6 - k + across, 6 : 6 + depth_cells]
        )
        total = total + coefs[k] * (
            padded[:, :, 6 : 6 + across, 6 + k : 6 + k + depth_cells]
            + padded[:, :, 6 : 6 + across, 6 - k : 6 - k + depth_cells]
        )
    return -2.0 * total + potential[None] * orbital_field


def combine_kernel(scale, with_base, *refs):
    if with_base:
        local_ref, own_ref, before_ref, after_ref, base_ref, out_ref = refs
    else:
        local_ref, own_ref, before_ref, after_ref, out_ref = refs
    width = before_ref.shape[1]
    planes_own = own_ref.shape[1]

    def plane(q):
        if q < 0:
            return before_ref[:, width + q]
        if q >= planes_own:
            return after_ref[:, q - planes_own]
        return own_ref[:, q]

    for p in range(planes_own):
        acc = coefs[1] * (plane(p + 1) + plane(p - 1))
        for k in range(2, 7):
            acc = acc + coefs[k] * (plane(p + k) + plane(p - k))
        value = local_ref[:, p] - 2.0 * acc
        value = (value - centre * own_ref[:, p]) * (scale / radius)
        if with_base:
            value = value - base_ref[:, p]
        out_ref[:, p] = value


def filter_step(
    local, orbital_field, before, after, scale, base=None, start=0, count=None, base_start=0, halo_start=None
):
    count = orbital_field.shape[0] if count is None else count
    halo_start = start if halo_start is None else halo_start
    aligned = all(value % 8 == 0 for value in (count, start, base_start, halo_start))
    block_rows = 8 if aligned else 1
    offset = start // block_rows
    halo_offset = halo_start // block_rows
    base_offset = base_start // block_rows
    block = (block_rows,) + orbital_field.shape[1:]
    halo_block = (block_rows,) + before.shape[1:]
    spec = pl.BlockSpec(block, lambda i: (i + offset, 0, 0, 0))
    halo_spec = pl.BlockSpec(halo_block, lambda i: (i + halo_offset, 0, 0, 0))
    operands = [local, orbital_field, before, after]
    specs = [spec, spec, halo_spec, halo_spec]
    if base is not None:
        operands.append(base)
        specs.append(pl.BlockSpec(block, lambda i: (i + base_offset, 0, 0, 0)))
    return pl.pallas_call(
        functools.partial(combine_kernel, scale, base is not None),
        grid=(count // block_rows,),
        in_specs=specs,
        out_specs=pl.BlockSpec(block, lambda i: (i, 0, 0, 0)),
        out_shape=jax.ShapeDtypeStruct((count,) + orbital_field.shape[1:], jnp.float32),
    )(*operands)


def spread_cells(filtered):
    rows = filtered.shape[0]
    parts = lax.axis_size("orb")
    lanes = filtered.shape[3]
    rows_per_part = filtered.shape[1] * filtered.shape[2] // parts
    chunks = filtered.reshape(rows, parts, rows_per_part, lanes)
    return lax.all_to_all(chunks, "orb", 1, 0, tiled=True).reshape(parts, rows, rows_per_part, lanes)


def gram_matrix(left_rows, right_rows):
    return lax.dot_general(
        left_rows,
        right_rows,
        (((1, 2), (1, 2)), ((), ())),
        precision=matmul_precision,
        preferred_element_type=jnp.float32,
    )


def apply_rows(inverse, source_rows):
    return lax.dot_general(
        inverse,
        source_rows,
        (((0,), (0,)), ((), ())),
        precision=matmul_precision,
        preferred_element_type=jnp.float32,
    )


def mix_rows(weights, source_rows):
    return lax.dot_general(
        weights,
        source_rows,
        (((1,), (0,)), ((), ())),
        precision=matmul_precision,
        preferred_element_type=jnp.float32,
    )


def group_round(value, axis, stride, radix):
    size = lax.axis_size(axis)
    position = (lax.axis_index(axis) // stride) % radix
    received = [value]
    for shift in range(1, radix):
        pairs = []
        for i in range(size):
            p = (i // stride) % radix
            pairs.append((i, i + ((p + shift) % radix - p) * stride))
        received.append(lax.ppermute(value, axis, pairs))
    total = None
    for q in range(radix):
        choice = (position - q) % radix
        term = received[0]
        for shift in range(1, radix):
            term = jnp.where(choice == shift, received[shift], term)
        total = term if total is None else total + term
    return total


def exchange_sum(value, axis):
    size = lax.axis_size(axis)
    if size & (size - 1):
        return lax.psum(value, axis)
    stride = 1
    if size.bit_length() % 2 == 0:
        value = group_round(value, axis, 1, 2)
        stride = 2
    while stride < size:
        value = group_round(value, axis, stride, 4)
        stride *= 4
    return value


def cell_sum(value):
    return exchange_sum(exchange_sum(value, "grid"), "orb")


def eliminate_kernel(source_ref, result_ref):
    result_ref[...] = source_ref[...]
    rows, width = result_ref.shape
    lanes = lax.broadcasted_iota(jnp.int32, (1, width), 1)
    cols = lax.broadcasted_iota(jnp.int32, (rows, width), 1)
    row_ids = lax.broadcasted_iota(jnp.int32, (rows, 1), 0)

    def column_step(column, carry):
        current = result_ref[pl.ds(column, 1), :]
        pivot_value = jnp.sum(jnp.where(lanes == column, current, 0.0), axis=1, keepdims=True)
        inv_root = lax.rsqrt(pivot_value)
        scaled = jnp.where(lanes >= column, current, 0.0) * inv_root
        whole = result_ref[...]
        below = jnp.sum(jnp.where(cols == column, whole, 0.0), axis=1, keepdims=True) * inv_root
        below = jnp.where(row_ids > column, below, 0.0)
        whole = whole - below * scaled
        result_ref[...] = jnp.where(row_ids == column, scaled, whole)
        return carry

    lax.fori_loop(0, rows, column_step, 0)


def eliminate(matrix, extra):
    source = jnp.concatenate([matrix, extra], axis=1)
    return pl.pallas_call(
        eliminate_kernel,
        out_shape=jax.ShapeDtypeStruct(source.shape, jnp.float32),
    )(source)


def factorize(rows_block, inv_cells):
    panel_rows = rows_block.shape[0] // 2
    leading = cell_sum(gram_matrix(rows_block[:panel_rows], rows_block)) * inv_cells
    eye = jnp.eye(panel_rows, dtype=jnp.float32)
    first = eliminate(leading, eye)
    first_r = first[:, :panel_rows]
    coupling = first[:, panel_rows : 2 * panel_rows]
    first_lower_inv = first[:, 2 * panel_rows :]
    first_q = mix_rows(first_lower_inv, rows_block[:panel_rows])
    remainder = rows_block[panel_rows:] - apply_rows(coupling, first_q)
    trailing = cell_sum(gram_matrix(remainder, remainder)) * inv_cells
    second = eliminate(trailing, eye)
    second_r = second[:, :panel_rows]
    second_lower_inv = second[:, panel_rows:]
    upper_rows = jnp.concatenate([first_r, coupling], axis=1)
    lower_rows = jnp.concatenate(
        [jnp.zeros((second_r.shape[0], panel_rows), jnp.float32), second_r], axis=1
    )
    triangle = jnp.concatenate([upper_rows, lower_rows], axis=0)
    return triangle, first_q, second_lower_inv, remainder


def local(orbital_block, potential):
    orb_rows = orbital_block.shape[0]
    half = orb_rows // 2
    local_part = local_terms(orbital_block, potential)
    before_0, after_0 = halo_planes(orbital_block[:half], "grid", 6)
    local_part, before_0, after_0 = lax.optimization_barrier((local_part, before_0, after_0))
    second_rows, before_0, after_0 = lax.optimization_barrier((orbital_block[half:], before_0, after_0))
    before_1, after_1 = halo_planes(second_rows, "grid", 6)
    first_a = filter_step(local_part, orbital_block, before_0, after_0, 1.0, start=0, count=half)
    before_1, after_1 = lax.optimization_barrier((before_1, after_1))
    first_b = filter_step(
        local_part, orbital_block, before_1, after_1, 1.0, start=half, count=orb_rows - half, halo_start=0
    )
    before_a, after_a = halo_planes(first_a, "grid", 6)
    local_a = local_terms(first_a, potential)
    local_a, before_a, after_a, first_b = lax.optimization_barrier((local_a, before_a, after_a, first_b))
    before_b, after_b = halo_planes(first_b, "grid", 6)
    filtered_a = filter_step(local_a, first_a, before_a, after_a, 2.0, base=orbital_block)
    spread_a = spread_cells(filtered_a)
    local_b = local_terms(first_b, potential)
    local_b, before_b, after_b = lax.optimization_barrier((local_b, before_b, after_b))
    filtered_b = lax.optimization_barrier(
        filter_step(local_b, first_b, before_b, after_b, 2.0, base=orbital_block, base_start=half)
    )
    spread_b = spread_cells(filtered_b)
    parts, _, rows_per_part, lanes = spread_a.shape
    spread = jnp.stack([spread_a, spread_b], axis=1).reshape(-1, rows_per_part, lanes)
    inv_cells = 1.0 / (lax.axis_size("grid") * parts * rows_per_part * lanes)
    triangle, first_q, second_lower_inv, remainder = factorize(spread, inv_cells)
    second_q = mix_rows(second_lower_inv, remainder)
    orbitals = jnp.concatenate([first_q, second_q], axis=0)
    orbitals = orbitals.reshape(orbitals.shape[0], 1, rows_per_part, lanes)
    orbitals = lax.all_to_all(orbitals, "orb", 0, 1, tiled=True)
    return (orbitals.reshape(orbital_block.shape), triangle)


def solution(mesh):
    in_specs = (P("orb", "grid", None, None), P("grid", None, None))
    out_specs = (P("orb", "grid", None, None), P())
    return jax.shard_map(local, mesh=mesh, in_specs=in_specs, out_specs=out_specs, check_vma=False)
```

```python
import functools

import jax
import jax.numpy as jnp
from jax import lax
from jax.experimental import pallas as pl
from jax.experimental.pallas import tpu as pltpu
from jax.sharding import PartitionSpec as P

coefs = (
    -5369.0 / 1800.0,
    12.0 / 7.0,
    -15.0 / 56.0,
    10.0 / 189.0,
    -1.0 / 112.0,
    2.0 / 1925.0,
    -1.0 / 16632.0,
)
centre = 23.5
radius = 19.5
matmul_precision = lax.Precision.HIGH


def halo_planes(value, axis, width):
    size, length = (lax.axis_size(axis), value.shape[1])
    up = [(i, (i + 1) % size) for i in range(size - 1)]
    down = [(j, i) for i, j in up]
    last = lax.slice_in_dim(value, length - width, length, axis=1)
    first = lax.slice_in_dim(value, 0, width, axis=1)
    before = lax.ppermute(last, axis, up)
    after = lax.ppermute(first, axis, down)
    return before, after


def local_terms(orbital_field, potential):
    across = orbital_field.shape[2]
    depth_cells = orbital_field.shape[3]
    padded = jnp.pad(orbital_field, ((0, 0), (0, 0), (6, 6), (6, 6)))
    total = 3.0 * coefs[0] * orbital_field
    for k in range(1, 7):
        total = total + coefs[k] * (
            padded[:, :, 6 + k : 6 + k + across, 6 : 6 + depth_cells]
            + padded[:, :, 6 - k : 6 - k + across, 6 : 6 + depth_cells]
        )
        total = total + coefs[k] * (
            padded[:, :, 6 : 6 + across, 6 + k : 6 + k + depth_cells]
            + padded[:, :, 6 : 6 + across, 6 - k : 6 - k + depth_cells]
        )
    return -2.0 * total + potential[None] * orbital_field


def combine_kernel(scale, with_base, *refs):
    if with_base:
        local_ref, own_ref, before_ref, after_ref, base_ref, out_ref = refs
    else:
        local_ref, own_ref, before_ref, after_ref, out_ref = refs
    width = before_ref.shape[1]
    planes_own = own_ref.shape[1]

    def plane(q):
        if q < 0:
            return before_ref[:, width + q]
        if q >= planes_own:
            return after_ref[:, q - planes_own]
        return own_ref[:, q]

    for p in range(planes_own):
        acc = coefs[1] * (plane(p + 1) + plane(p - 1))
        for k in range(2, 7):
            acc = acc + coefs[k] * (plane(p + k) + plane(p - k))
        value = local_ref[:, p] - 2.0 * acc
        value = scale * (value - centre * own_ref[:, p]) / radius
        if with_base:
            value = value - base_ref[:, p]
        out_ref[:, p] = value


def filter_step(
    local, orbital_field, before, after, scale, base=None, start=0, count=None, base_start=0, halo_start=None
):
    count = orbital_field.shape[0] if count is None else count
    halo_start = start if halo_start is None else halo_start
    aligned = all(value % 8 == 0 for value in (count, start, base_start, halo_start))
    block_rows = 8 if aligned else 1
    offset = start // block_rows
    halo_offset = halo_start // block_rows
    base_offset = base_start // block_rows
    block = (block_rows,) + orbital_field.shape[1:]
    halo_block = (block_rows,) + before.shape[1:]
    spec = pl.BlockSpec(block, lambda i: (i + offset, 0, 0, 0))
    halo_spec = pl.BlockSpec(halo_block, lambda i: (i + halo_offset, 0, 0, 0))
    operands = [local, orbital_field, before, after]
    specs = [spec, spec, halo_spec, halo_spec]
    if base is not None:
        operands.append(base)
        specs.append(pl.BlockSpec(block, lambda i: (i + base_offset, 0, 0, 0)))
    return pl.pallas_call(
        functools.partial(combine_kernel, scale, base is not None),
        grid=(count // block_rows,),
        in_specs=specs,
        out_specs=pl.BlockSpec(block, lambda i: (i, 0, 0, 0)),
        out_shape=jax.ShapeDtypeStruct((count,) + orbital_field.shape[1:], jnp.float32),
    )(*operands)


def spread_cells(filtered):
    rows = filtered.shape[0]
    parts = lax.axis_size("orb")
    lanes = filtered.shape[3]
    rows_per_part = filtered.shape[1] * filtered.shape[2] // parts
    chunks = filtered.reshape(rows, parts, rows_per_part, lanes)
    return lax.all_to_all(chunks, "orb", 1, 0, tiled=True).reshape(parts, rows, rows_per_part, lanes)


def gram_matrix(left_rows, right_rows):
    return lax.dot_general(
        left_rows,
        right_rows,
        (((1, 2), (1, 2)), ((), ())),
        precision=matmul_precision,
        preferred_element_type=jnp.float32,
    )


def apply_rows(inverse, source_rows):
    return lax.dot_general(
        inverse,
        source_rows,
        (((0,), (0,)), ((), ())),
        precision=matmul_precision,
        preferred_element_type=jnp.float32,
    )


def mix_rows(weights, source_rows):
    return lax.dot_general(
        weights,
        source_rows,
        (((1,), (0,)), ((), ())),
        precision=matmul_precision,
        preferred_element_type=jnp.float32,
    )


def group_round(value, axis, stride, radix):
    size = lax.axis_size(axis)
    position = (lax.axis_index(axis) // stride) % radix
    received = [value]
    for shift in range(1, radix):
        pairs = []
        for i in range(size):
            p = (i // stride) % radix
            pairs.append((i, i + ((p + shift) % radix - p) * stride))
        received.append(lax.ppermute(value, axis, pairs))
    total = None
    for q in range(radix):
        choice = (position - q) % radix
        term = received[0]
        for shift in range(1, radix):
            term = jnp.where(choice == shift, received[shift], term)
        total = term if total is None else total + term
    return total


def exchange_sum(value, axis):
    size = lax.axis_size(axis)
    if size & (size - 1):
        return lax.psum(value, axis)
    stride = 1
    if size.bit_length() % 2 == 0:
        value = group_round(value, axis, 1, 2)
        stride = 2
    while stride < size:
        value = group_round(value, axis, stride, 4)
        stride *= 4
    return value


def cell_sum(value):
    return exchange_sum(exchange_sum(value, "grid"), "orb")


def eliminate_kernel(source_ref, result_ref):
    result_ref[...] = source_ref[...]
    rows, width = result_ref.shape
    lanes = lax.broadcasted_iota(jnp.int32, (1, width), 1)
    cols = lax.broadcasted_iota(jnp.int32, (rows, width), 1)
    row_ids = lax.broadcasted_iota(jnp.int32, (rows, 1), 0)

    def column_step(column, carry):
        current = result_ref[pl.ds(column, 1), :]
        pivot_value = jnp.sum(jnp.where(lanes == column, current, 0.0), axis=1, keepdims=True)
        inv_root = lax.rsqrt(pivot_value)
        scaled = jnp.where(lanes >= column, current, 0.0) * inv_root
        whole = result_ref[...]
        below = jnp.sum(jnp.where(cols == column, whole, 0.0), axis=1, keepdims=True) * inv_root
        below = jnp.where(row_ids > column, below, 0.0)
        whole = whole - below * scaled
        result_ref[...] = jnp.where(row_ids == column, scaled, whole)
        return carry

    lax.fori_loop(0, rows, column_step, 0, unroll=2)


def eliminate(matrix, extra):
    source = jnp.concatenate([matrix, extra], axis=1)
    return pl.pallas_call(
        eliminate_kernel,
        out_shape=jax.ShapeDtypeStruct(source.shape, jnp.float32),
    )(source)


def factorize(rows_block, inv_cells):
    panel_rows = rows_block.shape[0] // 2
    leading = cell_sum(gram_matrix(rows_block[:panel_rows], rows_block)) * inv_cells
    eye = jnp.eye(panel_rows, dtype=jnp.float32)
    first = eliminate(leading, eye)
    first_r = first[:, :panel_rows]
    coupling = first[:, panel_rows : 2 * panel_rows]
    first_lower_inv = first[:, 2 * panel_rows :]
    first_q = mix_rows(first_lower_inv, rows_block[:panel_rows])
    remainder = rows_block[panel_rows:] - apply_rows(coupling, first_q)
    trailing = cell_sum(gram_matrix(remainder, remainder)) * inv_cells
    second = eliminate(trailing, eye)
    second_r = second[:, :panel_rows]
    second_lower_inv = second[:, panel_rows:]
    upper_rows = jnp.concatenate([first_r, coupling], axis=1)
    lower_rows = jnp.concatenate(
        [jnp.zeros((second_r.shape[0], panel_rows), jnp.float32), second_r], axis=1
    )
    triangle = jnp.concatenate([upper_rows, lower_rows], axis=0)
    return triangle, first_q, second_lower_inv, remainder


def local(orbital_block, potential):
    orb_rows = orbital_block.shape[0]
    half = orb_rows // 2
    local_part = local_terms(orbital_block, potential)
    before_0, after_0 = halo_planes(orbital_block[:half], "grid", 6)
    local_part, before_0, after_0 = lax.optimization_barrier((local_part, before_0, after_0))
    second_rows, before_0, after_0 = lax.optimization_barrier((orbital_block[half:], before_0, after_0))
    before_1, after_1 = halo_planes(second_rows, "grid", 6)
    first_a = filter_step(local_part, orbital_block, before_0, after_0, 1.0, start=0, count=half)
    before_1, after_1 = lax.optimization_barrier((before_1, after_1))
    first_b = filter_step(
        local_part, orbital_block, before_1, after_1, 1.0, start=half, count=orb_rows - half, halo_start=0
    )
    before_a, after_a = halo_planes(first_a, "grid", 6)
    local_a = local_terms(first_a, potential)
    local_a, before_a, after_a, first_b = lax.optimization_barrier((local_a, before_a, after_a, first_b))
    before_b, after_b = halo_planes(first_b, "grid", 6)
    filtered_a = filter_step(local_a, first_a, before_a, after_a, 2.0, base=orbital_block)
    spread_a = spread_cells(filtered_a)
    local_b = local_terms(first_b, potential)
    local_b, before_b, after_b = lax.optimization_barrier((local_b, before_b, after_b))
    filtered_b = lax.optimization_barrier(
        filter_step(local_b, first_b, before_b, after_b, 2.0, base=orbital_block, base_start=half)
    )
    spread_b = spread_cells(filtered_b)
    parts, _, rows_per_part, lanes = spread_a.shape
    spread = jnp.stack([spread_a, spread_b], axis=1).reshape(-1, rows_per_part, lanes)
    inv_cells = 1.0 / (lax.axis_size("grid") * parts * rows_per_part * lanes)
    triangle, first_q, second_lower_inv, remainder = factorize(spread, inv_cells)
    second_q = mix_rows(second_lower_inv, remainder)
    orbitals = jnp.concatenate([first_q, second_q], axis=0)
    orbitals = orbitals.reshape(orbitals.shape[0], 1, rows_per_part, lanes)
    orbitals = lax.all_to_all(orbitals, "orb", 0, 1, tiled=True)
    return (orbitals.reshape(orbital_block.shape), triangle)


def solution(mesh):
    in_specs = (P("orb", "grid", None, None), P("grid", None, None))
    out_specs = (P("orb", "grid", None, None), P())
    return jax.shard_map(local, mesh=mesh, in_specs=in_specs, out_specs=out_specs, check_vma=False)
```
